256 devices in a mesh: gx: 64 (over y, z, core), gz: 4 (over x).
Axes of the slice: x: 4, y: 4, z: 8, core: 2. Of those that a mesh axis runs over, the one named last changes fastest.
Arguments:
- field: float32 [4, 4, 512, 8192], P(None, 'gz', None, 'gx'), may hold values from -6 to 6
- drop_cell: int32 [1048576], P(('gx', 'gz')), may hold values from 0 to 65535
- drop_plane: int32 [1048576], P(('gx', 'gz')), may hold values from 0 to 3
- drop_rate: float32 [2, 1048576], P(None, ('gx', 'gz')), may hold values from -8 to 8
- diffusivity: float32 [4], replicated, may hold values from 0.25 to 4
- wall_eigen: float32 [512], replicated, may hold values from 0.05 to 2
- basis_part: float32 [512, 512], replicated, may hold values from -0.125 to 0.125
- dual_part: float32 [512, 512], replicated, may hold values from -0.125 to 0.125
- bulk_shift: float32 [1], replicated, may hold values from 2.2 to 2.8
Outputs:
- new_field: float32 [4, 4, 512, 8192], P(None, 'gz', None, 'gx')
The draws below stay inside these ranges and needn't reach their ends.
All inputs are finite; a program needn't handle non-finite values.
Results may differ from the reference program's by a relative error of at most 0.0001.
Values sent between devices are 32-bit elements; how exact they have to be, the bound alone decides.
No kernel may reach another device: no remote copies, remote signals or barrier semaphores. Data moves between devices by JAX's collectives and lax.ppermute only.
A program may use at most 64 MiB of HBM per device.

```python
import math
import jax
import jax.numpy as jnp
from jax import lax

F = 4
Y = 512
XD = 128
NX = 8192
PLANES = 4
SLAB_DROPS = 16384
DROPS = 1048576


def with_ends(entries, rng, least, top_value):
    index_at = [jax.random.randint(jax.random.fold_in(rng, axis), (), 0, length) for axis, length in enumerate(entries.shape)]
    main_axis = entries.shape.index(max(entries.shape))
    neighbour = index_at[:main_axis] + [(index_at[main_axis] + 1) % entries.shape[main_axis]] + index_at[main_axis + 1:]
    return entries.at[tuple(index_at)].set(least).at[tuple(neighbour)].set(top_value)


def block_levels(key, dims, shards, smallest, top_value):
    loudness = 1.0
    for axis_at, shards_of in shards:
        heights = jax.random.uniform(jax.random.fold_in(jax.random.fold_in(key, 6), axis_at), (shards_of,), jnp.float32, smallest / len(shards), top_value / len(shards))
        loudness = loudness * jnp.repeat(jnp.exp(heights), dims[axis_at] // shards_of).reshape((-1,) + (1,) * (len(dims) - 1 - axis_at))
    return loudness


def gaussian(stream_key, shape, width, bound, pieces=(), kind=jnp.bfloat16):
    result = width * jax.random.normal(stream_key, shape, jnp.float32)
    if pieces:
        result = result * block_levels(stream_key, shape, pieces, -0.22, 0.18)
    return jnp.clip(result, -bound, bound).astype(kind)


def setup_inputs(seed: int = 0) -> dict:
    key_of = jax.random.split(jax.random.key(seed), 10)
    return {
        "field": gaussian(key_of[0], (F, PLANES, Y, NX), 1.0, 6.0, ((1, 4), (3, 64)), jnp.float32),
        "drop_cell": with_ends(jax.random.randint(key_of[1], (DROPS,), 0, Y * XD), jax.random.fold_in(key_of[1], 1), 0, (Y * XD) - 1).astype(jnp.int32),
        "drop_plane": with_ends(jax.random.randint(key_of[2], (DROPS,), 0, PLANES), jax.random.fold_in(key_of[2], 1), 0, PLANES - 1).astype(jnp.int32),
        "drop_rate": gaussian(key_of[3], (2, DROPS), 2.0, 8.0, ((1, 256),), jnp.float32),
        "diffusivity": jnp.clip(jnp.exp(jax.random.uniform(key_of[4], (F,), jnp.float32, math.log(0.25), math.log(4.0))), 0.25, 4.0),
        "wall_eigen": jnp.clip(jnp.exp(jax.random.uniform(key_of[5], (Y,), jnp.float32, math.log(0.05), math.log(2.0))), 0.05, 2.0),
        "basis_part": gaussian(key_of[6], (Y, Y), (4 * Y) ** -0.5, 0.125, (), jnp.float32),
        "dual_part": gaussian(key_of[7], (Y, Y), (4 * Y) ** -0.5, 0.125, (), jnp.float32),
        "bulk_shift": jnp.clip(jax.random.uniform(key_of[8], (1,), jnp.float32, 2.2, 2.8), 2.2, 2.8),
    }


def reference(field, drop_cell, drop_plane, drop_rate, diffusivity, wall_eigen, basis_part, dual_part, bulk_shift):
    droplet_index = jnp.arange(DROPS, dtype=jnp.int32)
    slab_index = droplet_index // SLAB_DROPS
    column_index = slab_index * XD + drop_cell % XD
    height_index = drop_cell // XD
    flat_cell = ((drop_plane * Y + height_index) * NX + column_index).astype(jnp.int32)
    source = jnp.stack([jax.ops.segment_sum(drop_rate[component], flat_cell, num_segments=PLANES * Y * NX) for component in range(2)])
    source = source.reshape(2, PLANES, Y, NX)
    right_side = jnp.concatenate([field[:2], field[2:] + source], axis=0)
    identity = jnp.eye(Y, dtype=jnp.float32)
    dual_full = identity + dual_part
    basis_full = identity + basis_part
    mode_index = jnp.arange(NX, dtype=jnp.int32)
    folded = jnp.minimum(mode_index, NX - mode_index).astype(jnp.float32)
    wavenumber = (2.0 * math.pi / NX) * folded
    signed = jnp.where(2 * mode_index >= NX, mode_index - NX, mode_index).astype(jnp.float32)
    travel = (2.0 * math.pi / NX) * signed * bulk_shift[0]
    results = []
    for field_number in range(F):
        projected = jnp.einsum('ay,zyx->zax', dual_full, right_side[field_number], precision=lax.Precision.HIGHEST)
        spectrum = jnp.fft.fft(projected, axis=-1)
        growth = diffusivity[field_number] * (wall_eigen[:, None] + wavenumber[None, :] ** 2)
        damping = (1.0 - growth) / (1.0 + growth)
        factor = lax.complex(damping * jnp.cos(travel)[None, :], -damping * jnp.sin(travel)[None, :])
        filtered = jnp.real(jnp.fft.ifft(spectrum * factor[None], axis=-1))
        results.append(jnp.einsum('ya,zax->zyx', basis_full, filtered, precision=lax.Precision.HIGHEST))
    return jnp.stack(results)
```

```python
import math

import jax
import jax.numpy as jnp
from jax import lax
from jax.sharding import PartitionSpec as P

HI = lax.Precision.HIGHEST


def phase(numer, length):
    angle = 2.0 * math.pi / length * (numer % length).astype(jnp.float32)
    return jnp.cos(angle), jnp.sin(angle)


def per_device(
    field,
    drop_cell,
    drop_plane,
    drop_rate,
    diffusivity,
    wall_eigen,
    basis_part,
    dual_part,
    bulk_shift,
):
    field_count, plane_count, row_count, slab_width = field.shape
    gx_count = lax.axis_size("gx")
    gz_count = lax.axis_size("gz")
    total_cells = slab_width * gx_count
    plane_cells = row_count * slab_width
    rows_here = row_count // gx_count

    flat_cell = drop_plane * plane_cells + drop_cell
    partial_value = jnp.stack(
        [
            jax.ops.segment_sum(
                drop_rate[component], flat_cell, num_segments=plane_count * gz_count * plane_cells
            )
            for component in range(2)
        ]
    )
    partial_value = partial_value.reshape(2, plane_count * gz_count, row_count, slab_width)
    source = lax.psum_scatter(partial_value, "gz", scatter_dimension=1, tiled=True)
    right_side = jnp.concatenate([field[:2], field[2:] + source], axis=0)[:, 0]
    identity = jnp.eye(row_count, dtype=jnp.float32)
    projected = jnp.einsum("ay,fyx->fax", identity + dual_part, right_side, precision=HI)

    spread = lax.all_to_all(projected, "gx", 1, 1, tiled=True)
    spread = spread.reshape(field_count, gx_count, rows_here, slab_width)

    d_index = jnp.arange(gx_count, dtype=jnp.int32)
    j_index = jnp.arange(slab_width, dtype=jnp.int32)
    c64, s64 = phase(d_index[:, None] * d_index[None, :], gx_count)
    ct, st = phase(d_index[:, None] * j_index[None, :], total_cells)
    c128, s128 = phase(j_index[:, None] * j_index[None, :], slab_width)

    a_real = jnp.einsum("kd,fdaj->fkaj", c64, spread, precision=HI)
    a_imag = -jnp.einsum("kd,fdaj->fkaj", s64, spread, precision=HI)
    ct4 = ct[None, :, None, :]
    st4 = st[None, :, None, :]
    b_real = a_real * ct4 + a_imag * st4
    b_imag = a_imag * ct4 - a_real * st4
    joined = jnp.concatenate([b_real, b_imag], axis=-1)
    forward_table = jnp.concatenate(
        [jnp.concatenate([c128, -s128], axis=1), jnp.concatenate([s128, c128], axis=1)], axis=0
    )
    spec = jnp.einsum("fkaj,jm->fkam", joined, forward_table, precision=HI)
    spec_real = spec[..., :slab_width]
    spec_imag = spec[..., slab_width:]

    mode_index = d_index[:, None] + gx_count * j_index[None, :]
    folded = jnp.minimum(mode_index, total_cells - mode_index).astype(jnp.float32)
    wavenumber = 2.0 * math.pi / total_cells * folded
    position = lax.axis_index("gx")
    eigen_here = lax.dynamic_slice_in_dim(wall_eigen, position * rows_here, rows_here)
    growth = diffusivity[:, None, None, None] * (
        eigen_here[None, None, :, None] + (wavenumber**2)[None, :, None, :]
    )
    damping = (1.0 - growth) / (1.0 + growth)
    signed = jnp.where(2 * mode_index >= total_cells, mode_index - total_cells, mode_index).astype(
        jnp.float32
    )
    travel = 2.0 * math.pi / total_cells * signed * bulk_shift[0]
    cos_travel = jnp.cos(travel)[None, :, None, :]
    sin_travel = jnp.sin(travel)[None, :, None, :]
    factor_real = damping * cos_travel
    factor_imag = -damping * sin_travel
    turned_real = spec_real * factor_real - spec_imag * factor_imag
    turned_imag = spec_real * factor_imag + spec_imag * factor_real

    joined = jnp.concatenate([turned_real, turned_imag], axis=-1)
    inverse_table = jnp.concatenate(
        [jnp.concatenate([c128, s128], axis=1), jnp.concatenate([-s128, c128], axis=1)], axis=0
    )
    back = jnp.einsum("fkam,mj->fkaj", joined, inverse_table, precision=HI)
    back_real = back[..., :slab_width]
    back_imag = back[..., slab_width:]
    e_real = back_real * ct4 - back_imag * st4
    e_imag = back_real * st4 + back_imag * ct4
    filtered = (
        jnp.einsum("dk,fkaj->fdaj", c64, e_real, precision=HI)
        - jnp.einsum("dk,fkaj->fdaj", s64, e_imag, precision=HI)
    ) / total_cells

    filtered = filtered.reshape(field_count, row_count, slab_width)
    gathered = lax.all_to_all(filtered, "gx", 1, 1, tiled=True)
    result = jnp.einsum("ya,fax->fyx", identity + basis_part, gathered, precision=HI)
    return result[:, None]


def solution(mesh):
    in_specs = (
        P(None, "gz", None, "gx"),
        P(("gx", "gz")),
        P(("gx", "gz")),
        P(None, ("gx", "gz")),
        P(),
        P(),
        P(),
        P(),
        P(),
    )
    out_specs = P(None, "gz", None, "gx")
    return jax.shard_map(
        per_device, mesh=mesh, in_specs=in_specs, out_specs=out_specs, check_vma=False
    )
```

```python
import math

import jax
import jax.numpy as jnp
from jax import lax
from jax.experimental import pallas as pl
from jax.experimental.pallas import tpu as pltpu
from jax.sharding import PartitionSpec as P

HI = lax.Precision.HIGHEST


def phase(numer, length):
    angle = 2.0 * math.pi / length * (numer % length).astype(jnp.float32)
    return jnp.cos(angle), jnp.sin(angle)


PIECES = 3
CHUNK = 2048


def source_kernel(row_ref, col_ref, piece_ref, out_ref):
    step = pl.program_id(0)
    row_count = out_ref.shape[0]
    slab_width = out_ref.shape[1] // piece_ref.shape[0]
    chunk = row_ref.shape[1]
    rows = row_ref[...]
    cols = col_ref[...]
    row_hit = lax.broadcasted_iota(jnp.int32, (row_count, chunk), 0) == rows
    lhs = jnp.where(row_hit, 1.0, 0.0).astype(jnp.bfloat16)
    col_hit = lax.broadcasted_iota(jnp.int32, (slab_width, chunk), 0) == cols
    pieces = piece_ref[...]
    rhs = jnp.concatenate(
        [jnp.where(col_hit, pieces[p : p + 1, :], 0.0) for p in range(pieces.shape[0])], axis=0
    ).astype(jnp.bfloat16)
    part = lax.dot_general(
        lhs, rhs, (((1,), (1,)), ((), ())), preferred_element_type=jnp.float32
    )

    @pl.when(step == 0)
    def _():
        out_ref[...] = part

    @pl.when(step > 0)
    def _():
        out_ref[...] += part


def drop_source(cells, rates, row_count, slab_width):
    drops = cells.shape[0]
    pieces = []
    rest = rates
    for _ in range(PIECES):
        piece = lax.reduce_precision(rest, exponent_bits=8, mantissa_bits=7)
        pieces.append(piece)
        rest = rest - piece
    pieces = jnp.stack(pieces, axis=1).reshape(2 * PIECES, drops)
    rows = (cells // slab_width).reshape(1, drops)
    cols = (cells % slab_width).reshape(1, drops)
    width = 2 * PIECES * slab_width
    chunk = min(CHUNK, drops)
    summed = pl.pallas_call(
        source_kernel,
        grid=(drops // chunk,),
        in_specs=[
            pl.BlockSpec((1, chunk), lambda i: (0, i)),
            pl.BlockSpec((1, chunk), lambda i: (0, i)),
            pl.BlockSpec((2 * PIECES, chunk), lambda i: (0, i)),
        ],
        out_specs=pl.BlockSpec((row_count, width), lambda i: (0, 0)),
        out_shape=jax.ShapeDtypeStruct((row_count, width), jnp.float32),
        compiler_params=pltpu.CompilerParams(vmem_limit_bytes=48 * 1024 * 1024),
        cost_estimate=pl.CostEstimate(
            flops=2 * row_count * width * drops, transcendentals=0, bytes_accessed=4 * row_count * width
        ),
    )(rows, cols, pieces)
    summed = summed.reshape(row_count, 2, PIECES, slab_width)
    total = summed[:, :, 0]
    for p in range(1, PIECES):
        total = total + summed[:, :, p]
    return jnp.transpose(total, (1, 0, 2))


def per_device(
    field,
    drop_cell,
    drop_plane,
    drop_rate,
    diffusivity,
    wall_eigen,
    basis_part,
    dual_part,
    bulk_shift,
):
    field_count, plane_count, row_count, slab_width = field.shape
    gx_count = lax.axis_size("gx")
    gz_count = lax.axis_size("gz")
    total_cells = slab_width * gx_count
    plane_cells = row_count * slab_width
    rows_here = row_count // gx_count

    plane_here = lax.axis_index("gz")
    cells = lax.all_gather(drop_cell, "gz", tiled=True)
    planes = lax.all_gather(drop_plane, "gz", tiled=True)
    rates = lax.all_gather(drop_rate, "gz", axis=1, tiled=True)
    rates = jnp.where((planes == plane_here)[None, :], rates, 0.0)
    source = drop_source(cells, rates, row_count, slab_width)
    right_side = jnp.concatenate([field[:2], field[2:] + source[:, None]], axis=0)[:, 0]
    identity = jnp.eye(row_count, dtype=jnp.float32)
    projected = jnp.einsum("ay,fyx->fax", identity + dual_part, right_side, precision=HI)

    spread = lax.all_to_all(projected, "gx", 1, 1, tiled=True)
    spread = spread.reshape(field_count, gx_count, rows_here, slab_width)

    d_index = jnp.arange(gx_count, dtype=jnp.int32)
    j_index = jnp.arange(slab_width, dtype=jnp.int32)
    c64, s64 = phase(d_index[:, None] * d_index[None, :], gx_count)
    ct, st = phase(d_index[:, None] * j_index[None, :], total_cells)
    c128, s128 = phase(j_index[:, None] * j_index[None, :], slab_width)

    a_real = jnp.einsum("kd,fdaj->fkaj", c64, spread, precision=HI)
    a_imag = -jnp.einsum("kd,fdaj->fkaj", s64, spread, precision=HI)
    ct4 = ct[None, :, None, :]
    st4 = st[None, :, None, :]
    b_real = a_real * ct4 + a_imag * st4
    b_imag = a_imag * ct4 - a_real * st4
    joined = jnp.concatenate([b_real, b_imag], axis=-1)
    forward_table = jnp.concatenate(
        [jnp.concatenate([c128, -s128], axis=1), jnp.concatenate([s128, c128], axis=1)], axis=0
    )
    spec = jnp.einsum("fkaj,jm->fkam", joined, forward_table, precision=HI)
    spec_real = spec[..., :slab_width]
    spec_imag = spec[..., slab_width:]

    mode_index = d_index[:, None] + gx_count * j_index[None, :]
    folded = jnp.minimum(mode_index, total_cells - mode_index).astype(jnp.float32)
    wavenumber = 2.0 * math.pi / total_cells * folded
    position = lax.axis_index("gx")
    eigen_here = lax.dynamic_slice_in_dim(wall_eigen, position * rows_here, rows_here)
    growth = diffusivity[:, None, None, None] * (
        eigen_here[None, None, :, None] + (wavenumber**2)[None, :, None, :]
    )
    damping = (1.0 - growth) / (1.0 + growth)
    signed = jnp.where(2 * mode_index >= total_cells, mode_index - total_cells, mode_index).astype(
        jnp.float32
    )
    travel = 2.0 * math.pi / total_cells * signed * bulk_shift[0]
    cos_travel = jnp.cos(travel)[None, :, None, :]
    sin_travel = jnp.sin(travel)[None, :, None, :]
    factor_real = damping * cos_travel
    factor_imag = -damping * sin_travel
    turned_real = spec_real * factor_real - spec_imag * factor_imag
    turned_imag = spec_real * factor_imag + spec_imag * factor_real

    joined = jnp.concatenate([turned_real, turned_imag], axis=-1)
    inverse_table = jnp.concatenate(
        [jnp.concatenate([c128, s128], axis=1), jnp.concatenate([-s128, c128], axis=1)], axis=0
    )
    back = jnp.einsum("fkam,mj->fkaj", joined, inverse_table, precision=HI)
    back_real = back[..., :slab_width]
    back_imag = back[..., slab_width:]
    e_real = back_real * ct4 - back_imag * st4
    e_imag = back_real * st4 + back_imag * ct4
    filtered = (
        jnp.einsum("dk,fkaj->fdaj", c64, e_real, precision=HI)
        - jnp.einsum("dk,fkaj->fdaj", s64, e_imag, precision=HI)
    ) / total_cells

    filtered = filtered.reshape(field_count, row_count, slab_width)
    gathered = lax.all_to_all(filtered, "gx", 1, 1, tiled=True)
    result = jnp.einsum("ya,fax->fyx", identity + basis_part, gathered, precision=HI)
    return result[:, None]


def solution(mesh):
    in_specs = (
        P(None, "gz", None, "gx"),
        P(("gx", "gz")),
        P(("gx", "gz")),
        P(None, ("gx", "gz")),
        P(),
        P(),
        P(),
        P(),
        P(),
    )
    out_specs = P(None, "gz", None, "gx")
    return jax.shard_map(
        per_device, mesh=mesh, in_specs=in_specs, out_specs=out_specs, check_vma=False
    )
```

```python
import math

import jax
import jax.numpy as jnp
from jax import lax
from jax.experimental import pallas as pl
from jax.experimental.pallas import tpu as pltpu
from jax.sharding import PartitionSpec as P

HI = lax.Precision.HIGHEST


def phase(numer, length):
    angle = 2.0 * math.pi / length * (numer % length).astype(jnp.float32)
    return jnp.cos(angle), jnp.sin(angle)


PIECES = 3
CHUNK = 2048


def source_kernel(row_ref, col_ref, piece_ref, out_ref):
    step = pl.program_id(0)
    row_count = out_ref.shape[0]
    slab_width = out_ref.shape[1] // piece_ref.shape[0]
    chunk = row_ref.shape[1]
    rows = row_ref[...]
    cols = col_ref[...]
    row_hit = lax.broadcasted_iota(jnp.int32, (row_count, chunk), 0) == rows
    lhs = jnp.where(row_hit, 1.0, 0.0).astype(jnp.bfloat16)
    col_hit = lax.broadcasted_iota(jnp.int32, (slab_width, chunk), 0) == cols
    pieces = piece_ref[...]
    rhs = jnp.concatenate(
        [jnp.where(col_hit, pieces[p : p + 1, :], 0.0) for p in range(pieces.shape[0])], axis=0
    ).astype(jnp.bfloat16)
    part = lax.dot_general(
        lhs, rhs, (((1,), (1,)), ((), ())), preferred_element_type=jnp.float32
    )

    @pl.when(step == 0)
    def _():
        out_ref[...] = part

    @pl.when(step > 0)
    def _():
        out_ref[...] += part


def drop_source(cells, rates, row_count, slab_width):
    drops = cells.shape[0]
    pieces = []
    rest = rates
    for _ in range(PIECES):
        piece = lax.reduce_precision(rest, exponent_bits=8, mantissa_bits=7)
        pieces.append(piece)
        rest = rest - piece
    pieces = jnp.stack(pieces, axis=1).reshape(2 * PIECES, drops)
    rows = (cells // slab_width).reshape(1, drops)
    cols = (cells % slab_width).reshape(1, drops)
    width = 2 * PIECES * slab_width
    chunk = min(CHUNK, drops)
    summed = pl.pallas_call(
        source_kernel,
        grid=(drops // chunk,),
        in_specs=[
            pl.BlockSpec((1, chunk), lambda i: (0, i)),
            pl.BlockSpec((1, chunk), lambda i: (0, i)),
            pl.BlockSpec((2 * PIECES, chunk), lambda i: (0, i)),
        ],
        out_specs=pl.BlockSpec((row_count, width), lambda i: (0, 0)),
        out_shape=jax.ShapeDtypeStruct((row_count, width), jnp.float32),
        compiler_params=pltpu.CompilerParams(vmem_limit_bytes=48 * 1024 * 1024),
        cost_estimate=pl.CostEstimate(
            flops=2 * row_count * width * drops, transcendentals=0, bytes_accessed=4 * row_count * width
        ),
    )(rows, cols, pieces)
    summed = summed.reshape(row_count, 2, PIECES, slab_width)
    total = summed[:, :, 0]
    for p in range(1, PIECES):
        total = total + summed[:, :, p]
    return jnp.transpose(total, (1, 0, 2))


def per_device(
    field,
    drop_cell,
    drop_plane,
    drop_rate,
    diffusivity,
    wall_eigen,
    basis_part,
    dual_part,
    bulk_shift,
):
    field_count, plane_count, row_count, slab_width = field.shape
    gx_count = lax.axis_size("gx")
    gz_count = lax.axis_size("gz")
    total_cells = slab_width * gx_count
    plane_cells = row_count * slab_width
    rows_here = row_count // gx_count

    plane_here = lax.axis_index("gz")
    packed = jnp.concatenate(
        [(drop_plane * plane_cells + drop_cell).astype(jnp.float32)[None, :], drop_rate], axis=0
    )
    shares = [packed] + [
        lax.ppermute(packed, "gz", [(i, (i + shift) % gz_count) for i in range(gz_count)])
        for shift in range(1, gz_count)
    ]
    packed = jnp.concatenate(shares, axis=1)
    keys = packed[0].astype(jnp.int32)
    cells = keys % plane_cells
    planes = keys // plane_cells
    rates = jnp.where((planes == plane_here)[None, :], packed[1:], 0.0)
    source = drop_source(cells, rates, row_count, slab_width)
    right_side = jnp.concatenate([field[:2], field[2:] + source[:, None]], axis=0)[:, 0]
    identity = jnp.eye(row_count, dtype=jnp.float32)
    projected = jnp.einsum("ay,fyx->fax", identity + dual_part, right_side, precision=HI)

    spread = lax.all_to_all(projected, "gx", 1, 1, tiled=True)
    spread = spread.reshape(field_count, gx_count, rows_here, slab_width)

    d_index = jnp.arange(gx_count, dtype=jnp.int32)
    j_index = jnp.arange(slab_width, dtype=jnp.int32)
    c64, s64 = phase(d_index[:, None] * d_index[None, :], gx_count)
    ct, st = phase(d_index[:, None] * j_index[None, :], total_cells)
    c128, s128 = phase(j_index[:, None] * j_index[None, :], slab_width)

    a_real = jnp.einsum("kd,fdaj->fkaj", c64, spread, precision=HI)
    a_imag = -jnp.einsum("kd,fdaj->fkaj", s64, spread, precision=HI)
    ct4 = ct[None, :, None, :]
    st4 = st[None, :, None, :]
    b_real = a_real * ct4 + a_imag * st4
    b_imag = a_imag * ct4 - a_real * st4
    joined = jnp.concatenate([b_real, b_imag], axis=-1)
    forward_table = jnp.concatenate(
        [jnp.concatenate([c128, -s128], axis=1), jnp.concatenate([s128, c128], axis=1)], axis=0
    )
    spec = jnp.einsum("fkaj,jm->fkam", joined, forward_table, precision=HI)
    spec_real = spec[..., :slab_width]
    spec_imag = spec[..., slab_width:]

    mode_index = d_index[:, None] + gx_count * j_index[None, :]
    folded = jnp.minimum(mode_index, total_cells - mode_index).astype(jnp.float32)
    wavenumber = 2.0 * math.pi / total_cells * folded
    position = lax.axis_index("gx")
    eigen_here = lax.dynamic_slice_in_dim(wall_eigen, position * rows_here, rows_here)
    growth = diffusivity[:, None, None, None] * (
        eigen_here[None, None, :, None] + (wavenumber**2)[None, :, None, :]
    )
    damping = (1.0 - growth) / (1.0 + growth)
    signed = jnp.where(2 * mode_index >= total_cells, mode_index - total_cells, mode_index).astype(
        jnp.float32
    )
    travel = 2.0 * math.pi / total_cells * signed * bulk_shift[0]
    cos_travel = jnp.cos(travel)[None, :, None, :]
    sin_travel = jnp.sin(travel)[None, :, None, :]
    factor_real = damping * cos_travel
    factor_imag = -damping * sin_travel
    turned_real = spec_real * factor_real - spec_imag * factor_imag
    turned_imag = spec_real * factor_imag + spec_imag * factor_real

    joined = jnp.concatenate([turned_real, turned_imag], axis=-1)
    inverse_table = jnp.concatenate(
        [jnp.concatenate([c128, s128], axis=1), jnp.concatenate([-s128, c128], axis=1)], axis=0
    )
    back = jnp.einsum("fkam,mj->fkaj", joined, inverse_table, precision=HI)
    back_real = back[..., :slab_width]
    back_imag = back[..., slab_width:]
    e_real = back_real * ct4 - back_imag * st4
    e_imag = back_real * st4 + back_imag * ct4
    filtered = (
        jnp.einsum("dk,fkaj->fdaj", c64, e_real, precision=HI)
        - jnp.einsum("dk,fkaj->fdaj", s64, e_imag, precision=HI)
    ) / total_cells

    filtered = filtered.reshape(field_count, row_count, slab_width)
    gathered = lax.all_to_all(filtered, "gx", 1, 1, tiled=True)
    result = jnp.einsum("ya,fax->fyx", identity + basis_part, gathered, precision=HI)
    return result[:, None]


def solution(mesh):
    in_specs = (
        P(None, "gz", None, "gx"),
        P(("gx", "gz")),
        P(("gx", "gz")),
        P(None, ("gx", "gz")),
        P(),
        P(),
        P(),
        P(),
        P(),
    )
    out_specs = P(None, "gz", None, "gx")
    return jax.shard_map(
        per_device, mesh=mesh, in_specs=in_specs, out_specs=out_specs, check_vma=False
    )
```

```python
import math

import jax
import jax.numpy as jnp
from jax import lax
from jax.experimental import pallas as pl
from jax.experimental.pallas import tpu as pltpu
from jax.sharding import PartitionSpec as P

HI = lax.Precision.HIGHEST


def phase(numer, length):
    angle = 2.0 * math.pi / length * (numer % length).astype(jnp.float32)
    return jnp.cos(angle), jnp.sin(angle)


PIECES = 3
CHUNK = 2048


def source_kernel(row_ref, col_ref, piece_ref, out_ref):
    step = pl.program_id(0)
    row_count = out_ref.shape[0]
    slab_width = out_ref.shape[1] // piece_ref.shape[0]
    chunk = row_ref.shape[1]
    rows = row_ref[...]
    cols = col_ref[...]
    row_hit = lax.broadcasted_iota(jnp.int32, (row_count, chunk), 0) == rows
    lhs = jnp.where(row_hit, 1.0, 0.0).astype(jnp.bfloat16)
    col_hit = lax.broadcasted_iota(jnp.int32, (slab_width, chunk), 0) == cols
    pieces = piece_ref[...]
    rhs = jnp.concatenate(
        [jnp.where(col_hit, pieces[p : p + 1, :], 0.0) for p in range(pieces.shape[0])], axis=0
    ).astype(jnp.bfloat16)
    part = lax.dot_general(
        lhs, rhs, (((1,), (1,)), ((), ())), preferred_element_type=jnp.float32
    )

    @pl.when(step == 0)
    def _():
        out_ref[...] = part

    @pl.when(step > 0)
    def _():
        out_ref[...] += part


def drop_source(cells, rates, row_count, slab_width):
    drops = cells.shape[0]
    pieces = []
    rest = rates
    for _ in range(PIECES):
        piece = lax.reduce_precision(rest, exponent_bits=8, mantissa_bits=7)
        pieces.append(piece)
        rest = rest - piece
    pieces = jnp.stack(pieces, axis=1).reshape(2 * PIECES, drops)
    rows = (cells // slab_width).reshape(1, drops)
    cols = (cells % slab_width).reshape(1, drops)
    width = 2 * PIECES * slab_width
    chunk = min(CHUNK, drops)
    summed = pl.pallas_call(
        source_kernel,
        grid=(drops // chunk,),
        in_specs=[
            pl.BlockSpec((1, chunk), lambda i: (0, i)),
            pl.BlockSpec((1, chunk), lambda i: (0, i)),
            pl.BlockSpec((2 * PIECES, chunk), lambda i: (0, i)),
        ],
        out_specs=pl.BlockSpec((row_count, width), lambda i: (0, 0)),
        out_shape=jax.ShapeDtypeStruct((row_count, width), jnp.float32),
        compiler_params=pltpu.CompilerParams(vmem_limit_bytes=48 * 1024 * 1024),
        cost_estimate=pl.CostEstimate(
            flops=2 * row_count * width * drops, transcendentals=0, bytes_accessed=4 * row_count * width
        ),
    )(rows, cols, pieces)
    summed = summed.reshape(row_count, 2, PIECES, slab_width)
    total = summed[:, :, 0]
    for p in range(1, PIECES):
        total = total + summed[:, :, p]
    return jnp.transpose(total, (1, 0, 2))


def per_device(
    field,
    drop_cell,
    drop_plane,
    drop_rate,
    diffusivity,
    wall_eigen,
    basis_part,
    dual_part,
    bulk_shift,
):
    field_count, plane_count, row_count, slab_width = field.shape
    gx_count = lax.axis_size("gx")
    gz_count = lax.axis_size("gz")
    total_cells = slab_width * gx_count
    plane_cells = row_count * slab_width
    rows_here = row_count // gx_count

    plane_here = lax.axis_index("gz")
    packed = jnp.concatenate(
        [(drop_plane * plane_cells + drop_cell).astype(jnp.float32)[None, :], drop_rate], axis=0
    )
    shares = [packed] + [
        lax.ppermute(packed, "gz", [(i, (i + shift) % gz_count) for i in range(gz_count)])
        for shift in range(1, gz_count)
    ]
    packed = jnp.concatenate(shares, axis=1)
    keys = packed[0].astype(jnp.int32)
    cells = keys % plane_cells
    planes = keys // plane_cells
    rates = jnp.where((planes == plane_here)[None, :], packed[1:], 0.0)
    source = drop_source(cells, rates, row_count, slab_width)
    identity = jnp.eye(row_count, dtype=jnp.float32)
    dual_full = identity + dual_part
    basis_full = identity + basis_part
    position = lax.axis_index("gx")
    eigen_here = lax.dynamic_slice_in_dim(wall_eigen, position * rows_here, rows_here)
    tables = dft_tables(gx_count, slab_width)

    calm = filter_group(field[:2, 0], dual_full, basis_full, diffusivity[:2], eigen_here, bulk_shift, tables)
    fed = filter_group(
        field[2:, 0] + source, dual_full, basis_full, diffusivity[2:], eigen_here, bulk_shift, tables
    )
    return jnp.concatenate([calm, fed], axis=0)[:, None]


def dft_tables(gx_count, slab_width):
    total_cells = gx_count * slab_width
    d_index = jnp.arange(gx_count, dtype=jnp.int32)
    j_index = jnp.arange(slab_width, dtype=jnp.int32)
    c64, s64 = phase(d_index[:, None] * d_index[None, :], gx_count)
    ct, st = phase(d_index[:, None] * j_index[None, :], total_cells)
    c128, s128 = phase(j_index[:, None] * j_index[None, :], slab_width)
    forward_table = jnp.concatenate(
        [jnp.concatenate([c128, -s128], axis=1), jnp.concatenate([s128, c128], axis=1)], axis=0
    )
    inverse_table = jnp.concatenate(
        [jnp.concatenate([c128, s128], axis=1), jnp.concatenate([-s128, c128], axis=1)], axis=0
    )
    mode_index = d_index[:, None] + gx_count * j_index[None, :]
    return c64, s64, ct, st, forward_table, inverse_table, mode_index


def filter_group(right_side, dual_full, basis_full, diffusivity, eigen_here, bulk_shift, tables):
    c64, s64, ct, st, forward_table, inverse_table, mode_index = tables
    field_count, row_count, slab_width = right_side.shape
    gx_count = c64.shape[0]
    rows_here = row_count // gx_count
    total_cells = gx_count * slab_width
    projected = jnp.einsum("ay,fyx->fax", dual_full, right_side, precision=HI)

    spread = lax.all_to_all(projected, "gx", 1, 1, tiled=True)
    spread = spread.reshape(field_count, gx_count, rows_here, slab_width)

    a_real = jnp.einsum("kd,fdaj->fkaj", c64, spread, precision=HI)
    a_imag = -jnp.einsum("kd,fdaj->fkaj", s64, spread, precision=HI)
    ct4 = ct[None, :, None, :]
    st4 = st[None, :, None, :]
    b_real = a_real * ct4 + a_imag * st4
    b_imag = a_imag * ct4 - a_real * st4
    joined = jnp.concatenate([b_real, b_imag], axis=-1)
    spec = jnp.einsum("fkaj,jm->fkam", joined, forward_table, precision=HI)
    spec_real = spec[..., :slab_width]
    spec_imag = spec[..., slab_width:]

    folded = jnp.minimum(mode_index, total_cells - mode_index).astype(jnp.float32)
    wavenumber = 2.0 * math.pi / total_cells * folded
    growth = diffusivity[:, None, None, None] * (
        eigen_here[None, None, :, None] + (wavenumber**2)[None, :, None, :]
    )
    damping = (1.0 - growth) / (1.0 + growth)
    signed = jnp.where(2 * mode_index >= total_cells, mode_index - total_cells, mode_index).astype(
        jnp.float32
    )
    travel = 2.0 * math.pi / total_cells * signed * bulk_shift[0]
    cos_travel = jnp.cos(travel)[None, :, None, :]
    sin_travel = jnp.sin(travel)[None, :, None, :]
    factor_real = damping * cos_travel
    factor_imag = -damping * sin_travel
    turned_real = spec_real * factor_real - spec_imag * factor_imag
    turned_imag = spec_real * factor_imag + spec_imag * factor_real

    joined = jnp.concatenate([turned_real, turned_imag], axis=-1)
    back = jnp.einsum("fkam,mj->fkaj", joined, inverse_table, precision=HI)
    back_real = back[..., :slab_width]
    back_imag = back[..., slab_width:]
    e_real = back_real * ct4 - back_imag * st4
    e_imag = back_real * st4 + back_imag * ct4
    filtered = (
        jnp.einsum("dk,fkaj->fdaj", c64, e_real, precision=HI)
        - jnp.einsum("dk,fkaj->fdaj", s64, e_imag, precision=HI)
    ) / total_cells

    filtered = filtered.reshape(field_count, row_count, slab_width)
    gathered = lax.all_to_all(filtered, "gx", 1, 1, tiled=True)
    return jnp.einsum("ya,fax->fyx", basis_full, gathered, precision=HI)


def solution(mesh):
    in_specs = (
        P(None, "gz", None, "gx"),
        P(("gx", "gz")),
        P(("gx", "gz")),
        P(None, ("gx", "gz")),
        P(),
        P(),
        P(),
        P(),
        P(),
    )
    out_specs = P(None, "gz", None, "gx")
    return jax.shard_map(
        per_device, mesh=mesh, in_specs=in_specs, out_specs=out_specs, check_vma=False
    )
```

```python
import math

import jax
import jax.numpy as jnp
from jax import lax
from jax.experimental import pallas as pl
from jax.experimental.pallas import tpu as pltpu
from jax.sharding import PartitionSpec as P

HI = lax.Precision.HIGH


def phase(numer, length):
    angle = 2.0 * math.pi / length * (numer % length).astype(jnp.float32)
    return jnp.cos(angle), jnp.sin(angle)


PIECES = 3
CHUNK = 2048


def source_kernel(row_ref, col_ref, piece_ref, out_ref):
    step = pl.program_id(0)
    row_count = out_ref.shape[0]
    slab_width = out_ref.shape[1] // piece_ref.shape[0]
    chunk = row_ref.shape[1]
    rows = row_ref[...]
    cols = col_ref[...]
    row_hit = lax.broadcasted_iota(jnp.int32, (row_count, chunk), 0) == rows
    lhs = jnp.where(row_hit, 1.0, 0.0).astype(jnp.bfloat16)
    col_hit = lax.broadcasted_iota(jnp.int32, (slab_width, chunk), 0) == cols
    pieces = piece_ref[...]
    rhs = jnp.concatenate(
        [jnp.where(col_hit, pieces[p : p + 1, :], 0.0) for p in range(pieces.shape[0])], axis=0
    ).astype(jnp.bfloat16)
    part = lax.dot_general(
        lhs, rhs, (((1,), (1,)), ((), ())), preferred_element_type=jnp.float32
    )

    @pl.when(step == 0)
    def _():
        out_ref[...] = part

    @pl.when(step > 0)
    def _():
        out_ref[...] += part


def drop_source(cells, rates, row_count, slab_width):
    drops = cells.shape[0]
    pieces = []
    rest = rates
    for _ in range(PIECES):
        piece = lax.reduce_precision(rest, exponent_bits=8, mantissa_bits=7)
        pieces.append(piece)
        rest = rest - piece
    pieces = jnp.stack(pieces, axis=1).reshape(2 * PIECES, drops)
    rows = (cells // slab_width).reshape(1, drops)
    cols = (cells % slab_width).reshape(1, drops)
    width = 2 * PIECES * slab_width
    chunk = min(CHUNK, drops)
    summed = pl.pallas_call(
        source_kernel,
        grid=(drops // chunk,),
        in_specs=[
            pl.BlockSpec((1, chunk), lambda i: (0, i)),
            pl.BlockSpec((1, chunk), lambda i: (0, i)),
            pl.BlockSpec((2 * PIECES, chunk), lambda i: (0, i)),
        ],
        out_specs=pl.BlockSpec((row_count, width), lambda i: (0, 0)),
        out_shape=jax.ShapeDtypeStruct((row_count, width), jnp.float32),
        compiler_params=pltpu.CompilerParams(vmem_limit_bytes=48 * 1024 * 1024),
        cost_estimate=pl.CostEstimate(
            flops=2 * row_count * width * drops, transcendentals=0, bytes_accessed=4 * row_count * width
        ),
    )(rows, cols, pieces)
    summed = summed.reshape(row_count, 2, PIECES, slab_width)
    total = summed[:, :, 0]
    for p in range(1, PIECES):
        total = total + summed[:, :, p]
    return jnp.transpose(total, (1, 0, 2))


def per_device(
    field,
    drop_cell,
    drop_plane,
    drop_rate,
    diffusivity,
    wall_eigen,
    basis_part,
    dual_part,
    bulk_shift,
):
    field_count, plane_count, row_count, slab_width = field.shape
    gx_count = lax.axis_size("gx")
    gz_count = lax.axis_size("gz")
    total_cells = slab_width * gx_count
    plane_cells = row_count * slab_width
    rows_here = row_count // gx_count

    plane_here = lax.axis_index("gz")
    packed = jnp.concatenate(
        [(drop_plane * plane_cells + drop_cell).astype(jnp.float32)[None, :], drop_rate], axis=0
    )
    shares = [packed] + [
        lax.ppermute(packed, "gz", [(i, (i + shift) % gz_count) for i in range(gz_count)])
        for shift in range(1, gz_count)
    ]
    packed = jnp.concatenate(shares, axis=1)
    keys = packed[0].astype(jnp.int32)
    cells = keys % plane_cells
    planes = keys // plane_cells
    rates = jnp.where((planes == plane_here)[None, :], packed[1:], 0.0)
    source = drop_source(cells, rates, row_count, slab_width)
    right_side = jnp.concatenate([field[:2], field[2:] + source[:, None]], axis=0)[:, 0]
    identity = jnp.eye(row_count, dtype=jnp.float32)
    projected = jnp.einsum("ay,fyx->fax", identity + dual_part, right_side, precision=HI)

    spread = lax.all_to_all(projected, "gx", 1, 1, tiled=True)
    spread = spread.reshape(field_count, gx_count, rows_here, slab_width)

    d_index = jnp.arange(gx_count, dtype=jnp.int32)
    j_index = jnp.arange(slab_width, dtype=jnp.int32)
    c64, s64 = phase(d_index[:, None] * d_index[None, :], gx_count)
    ct, st = phase(d_index[:, None] * j_index[None, :], total_cells)
    c128, s128 = phase(j_index[:, None] * j_index[None, :], slab_width)

    a_real = jnp.einsum("kd,fdaj->fkaj", c64, spread, precision=HI)
    a_imag = -jnp.einsum("kd,fdaj->fkaj", s64, spread, precision=HI)
    ct4 = ct[None, :, None, :]
    st4 = st[None, :, None, :]
    b_real = a_real * ct4 + a_imag * st4
    b_imag = a_imag * ct4 - a_real * st4
    joined = jnp.concatenate([b_real, b_imag], axis=-1)
    forward_table = jnp.concatenate(
        [jnp.concatenate([c128, -s128], axis=1), jnp.concatenate([s128, c128], axis=1)], axis=0
    )
    spec = jnp.einsum("fkaj,jm->fkam", joined, forward_table, precision=HI)
    spec_real = spec[..., :slab_width]
    spec_imag = spec[..., slab_width:]

    mode_index = d_index[:, None] + gx_count * j_index[None, :]
    folded = jnp.minimum(mode_index, total_cells - mode_index).astype(jnp.float32)
    wavenumber = 2.0 * math.pi / total_cells * folded
    position = lax.axis_index("gx")
    eigen_here = lax.dynamic_slice_in_dim(wall_eigen, position * rows_here, rows_here)
    growth = diffusivity[:, None, None, None] * (
        eigen_here[None, None, :, None] + (wavenumber**2)[None, :, None, :]
    )
    damping = (1.0 - growth) / (1.0 + growth)
    signed = jnp.where(2 * mode_index >= total_cells, mode_index - total_cells, mode_index).astype(
        jnp.float32
    )
    travel = 2.0 * math.pi / total_cells * signed * bulk_shift[0]
    cos_travel = jnp.cos(travel)[None, :, None, :]
    sin_travel = jnp.sin(travel)[None, :, None, :]
    factor_real = damping * cos_travel
    factor_imag = -damping * sin_travel
    turned_real = spec_real * factor_real - spec_imag * factor_imag
    turned_imag = spec_real * factor_imag + spec_imag * factor_real

    joined = jnp.concatenate([turned_real, turned_imag], axis=-1)
    inverse_table = jnp.concatenate(
        [jnp.concatenate([c128, s128], axis=1), jnp.concatenate([-s128, c128], axis=1)], axis=0
    )
    back = jnp.einsum("fkam,mj->fkaj", joined, inverse_table, precision=HI)
    back_real = back[..., :slab_width]
    back_imag = back[..., slab_width:]
    e_real = back_real * ct4 - back_imag * st4
    e_imag = back_real * st4 + back_imag * ct4
    filtered = (
        jnp.einsum("dk,fkaj->fdaj", c64, e_real, precision=HI)
        - jnp.einsum("dk,fkaj->fdaj", s64, e_imag, precision=HI)
    ) / total_cells

    filtered = filtered.reshape(field_count, row_count, slab_width)
    gathered = lax.all_to_all(filtered, "gx", 1, 1, tiled=True)
    result = jnp.einsum("ya,fax->fyx", identity + basis_part, gathered, precision=HI)
    return result[:, None]


def solution(mesh):
    in_specs = (
        P(None, "gz", None, "gx"),
        P(("gx", "gz")),
        P(("gx", "gz")),
        P(None, ("gx", "gz")),
        P(),
        P(),
        P(),
        P(),
        P(),
    )
    out_specs = P(None, "gz", None, "gx")
    return jax.shard_map(
        per_device, mesh=mesh, in_specs=in_specs, out_specs=out_specs, check_vma=False
    )
```

```python
import math

import jax
import jax.numpy as jnp
from jax import lax
from jax.experimental import pallas as pl
from jax.experimental.pallas import tpu as pltpu
from jax.sharding import PartitionSpec as P

HI = lax.Precision.HIGH


def phase(numer, length):
    angle = 2.0 * math.pi / length * (numer % length).astype(jnp.float32)
    return jnp.cos(angle), jnp.sin(angle)


PIECES = 2
CHUNK = 2048


def source_kernel(row_ref, col_ref, piece_ref, out_ref):
    step = pl.program_id(0)
    row_count = out_ref.shape[0]
    slab_width = out_ref.shape[1] // piece_ref.shape[0]
    chunk = row_ref.shape[1]
    rows = row_ref[...]
    cols = col_ref[...]
    row_hit = lax.broadcasted_iota(jnp.int32, (row_count, chunk), 0) == rows
    lhs = jnp.where(row_hit, 1.0, 0.0).astype(jnp.bfloat16)
    col_hit = lax.broadcasted_iota(jnp.int32, (slab_width, chunk), 0) == cols
    pieces = piece_ref[...]
    rhs = jnp.concatenate(
        [jnp.where(col_hit, pieces[p : p + 1, :], 0.0) for p in range(pieces.shape[0])], axis=0
    ).astype(jnp.bfloat16)
    part = lax.dot_general(
        lhs, rhs, (((1,), (1,)), ((), ())), preferred_element_type=jnp.float32
    )

    @pl.when(step == 0)
    def _():
        out_ref[...] = part

    @pl.when(step > 0)
    def _():
        out_ref[...] += part


def drop_source(cells, rates, row_count, slab_width):
    drops = cells.shape[0]
    pieces = []
    rest = rates
    for _ in range(PIECES):
        piece = lax.reduce_precision(rest, exponent_bits=8, mantissa_bits=7)
        pieces.append(piece)
        rest = rest - piece
    pieces = jnp.stack(pieces, axis=1).reshape(2 * PIECES, drops)
    rows = (cells // slab_width).reshape(1, drops)
    cols = (cells % slab_width).reshape(1, drops)
    width = 2 * PIECES * slab_width
    chunk = min(CHUNK, drops)
    summed = pl.pallas_call(
        source_kernel,
        grid=(drops // chunk,),
        in_specs=[
            pl.BlockSpec((1, chunk), lambda i: (0, i)),
            pl.BlockSpec((1, chunk), lambda i: (0, i)),
            pl.BlockSpec((2 * PIECES, chunk), lambda i: (0, i)),
        ],
        out_specs=pl.BlockSpec((row_count, width), lambda i: (0, 0)),
        out_shape=jax.ShapeDtypeStruct((row_count, width), jnp.float32),
        compiler_params=pltpu.CompilerParams(vmem_limit_bytes=48 * 1024 * 1024),
        cost_estimate=pl.CostEstimate(
            flops=2 * row_count * width * drops, transcendentals=0, bytes_accessed=4 * row_count * width
        ),
    )(rows, cols, pieces)
    summed = summed.reshape(row_count, 2, PIECES, slab_width)
    total = summed[:, :, 0]
    for p in range(1, PIECES):
        total = total + summed[:, :, p]
    return jnp.transpose(total, (1, 0, 2))


def per_device(
    field,
    drop_cell,
    drop_plane,
    drop_rate,
    diffusivity,
    wall_eigen,
    basis_part,
    dual_part,
    bulk_shift,
):
    field_count, plane_count, row_count, slab_width = field.shape
    gx_count = lax.axis_size("gx")
    gz_count = lax.axis_size("gz")
    total_cells = slab_width * gx_count
    plane_cells = row_count * slab_width
    rows_here = row_count // gx_count

    plane_here = lax.axis_index("gz")
    packed = jnp.concatenate(
        [(drop_plane * plane_cells + drop_cell).astype(jnp.float32)[None, :], drop_rate], axis=0
    )
    shares = [packed] + [
        lax.ppermute(packed, "gz", [(i, (i + shift) % gz_count) for i in range(gz_count)])
        for shift in range(1, gz_count)
    ]
    packed = jnp.concatenate(shares, axis=1)
    keys = packed[0].astype(jnp.int32)
    cells = keys % plane_cells
    planes = keys // plane_cells
    rates = jnp.where((planes == plane_here)[None, :], packed[1:], 0.0)
    source = drop_source(cells, rates, row_count, slab_width)
    right_side = jnp.concatenate([field[:2], field[2:] + source[:, None]], axis=0)[:, 0]
    identity = jnp.eye(row_count, dtype=jnp.float32)
    projected = jnp.einsum("ay,fyx->fax", identity + dual_part, right_side, precision=HI)

    spread = lax.all_to_all(projected, "gx", 1, 1, tiled=True)
    spread = spread.reshape(field_count, gx_count, rows_here, slab_width)

    d_index = jnp.arange(gx_count, dtype=jnp.int32)
    j_index = jnp.arange(slab_width, dtype=jnp.int32)
    c64, s64 = phase(d_index[:, None] * d_index[None, :], gx_count)
    ct, st = phase(d_index[:, None] * j_index[None, :], total_cells)
    c128, s128 = phase(j_index[:, None] * j_index[None, :], slab_width)

    a_real = jnp.einsum("kd,fdaj->fkaj", c64, spread, precision=HI)
    a_imag = -jnp.einsum("kd,fdaj->fkaj", s64, spread, precision=HI)
    ct4 = ct[None, :, None, :]
    st4 = st[None, :, None, :]
    b_real = a_real * ct4 + a_imag * st4
    b_imag = a_imag * ct4 - a_real * st4
    joined = jnp.concatenate([b_real, b_imag], axis=-1)
    forward_table = jnp.concatenate(
        [jnp.concatenate([c128, -s128], axis=1), jnp.concatenate([s128, c128], axis=1)], axis=0
    )
    spec = jnp.einsum("fkaj,jm->fkam", joined, forward_table, precision=HI)
    spec_real = spec[..., :slab_width]
    spec_imag = spec[..., slab_width:]

    mode_index = d_index[:, None] + gx_count * j_index[None, :]
    folded = jnp.minimum(mode_index, total_cells - mode_index).astype(jnp.float32)
    wavenumber = 2.0 * math.pi / total_cells * folded
    position = lax.axis_index("gx")
    eigen_here = lax.dynamic_slice_in_dim(wall_eigen, position * rows_here, rows_here)
    growth = diffusivity[:, None, None, None] * (
        eigen_here[None, None, :, None] + (wavenumber**2)[None, :, None, :]
    )
    damping = (1.0 - growth) / (1.0 + growth)
    signed = jnp.where(2 * mode_index >= total_cells, mode_index - total_cells, mode_index).astype(
        jnp.float32
    )
    travel = 2.0 * math.pi / total_cells * signed * bulk_shift[0]
    cos_travel = jnp.cos(travel)[None, :, None, :]
    sin_travel = jnp.sin(travel)[None, :, None, :]
    factor_real = damping * cos_travel
    factor_imag = -damping * sin_travel
    turned_real = spec_real * factor_real - spec_imag * factor_imag
    turned_imag = spec_real * factor_imag + spec_imag * factor_real

    joined = jnp.concatenate([turned_real, turned_imag], axis=-1)
    inverse_table = jnp.concatenate(
        [jnp.concatenate([c128, s128], axis=1), jnp.concatenate([-s128, c128], axis=1)], axis=0
    )
    back = jnp.einsum("fkam,mj->fkaj", joined, inverse_table, precision=HI)
    back_real = back[..., :slab_width]
    back_imag = back[..., slab_width:]
    e_real = back_real * ct4 - back_imag * st4
    e_imag = back_real * st4 + back_imag * ct4
    filtered = (
        jnp.einsum("dk,fkaj->fdaj", c64, e_real, precision=HI)
        - jnp.einsum("dk,fkaj->fdaj", s64, e_imag, precision=HI)
    ) / total_cells

    filtered = filtered.reshape(field_count, row_count, slab_width)
    gathered = lax.all_to_all(filtered, "gx", 1, 1, tiled=True)
    result = jnp.einsum("ya,fax->fyx", identity + basis_part, gathered, precision=HI)
    return result[:, None]


def solution(mesh):
    in_specs = (
        P(None, "gz", None, "gx"),
        P(("gx", "gz")),
        P(("gx", "gz")),
        P(None, ("gx", "gz")),
        P(),
        P(),
        P(),
        P(),
        P(),
    )
    out_specs = P(None, "gz", None, "gx")
    return jax.shard_map(
        per_device, mesh=mesh, in_specs=in_specs, out_specs=out_specs, check_vma=False
    )
```

```python
import math

import jax
import jax.numpy as jnp
from jax import lax
from jax.experimental import pallas as pl
from jax.experimental.pallas import tpu as pltpu
from jax.sharding import PartitionSpec as P

HI = lax.Precision.HIGH


def phase(numer, length):
    angle = 2.0 * math.pi / length * (numer % length).astype(jnp.float32)
    return jnp.cos(angle), jnp.sin(angle)


PIECES = 2
CHUNK = 2048


def source_kernel(row_ref, col_ref, piece_ref, out_ref):
    step = pl.program_id(0)
    row_count = out_ref.shape[0]
    slab_width = out_ref.shape[1] // piece_ref.shape[0]
    chunk = row_ref.shape[1]
    rows = row_ref[...]
    cols = col_ref[...]
    row_hit = lax.broadcasted_iota(jnp.int32, (row_count, chunk), 0) == rows
    lhs = jnp.where(row_hit, 1.0, 0.0).astype(jnp.bfloat16)
    col_hit = lax.broadcasted_iota(jnp.int32, (slab_width, chunk), 0) == cols
    pieces = piece_ref[...]
    rhs = jnp.concatenate(
        [jnp.where(col_hit, pieces[p : p + 1, :], 0.0) for p in range(pieces.shape[0])], axis=0
    ).astype(jnp.bfloat16)
    part = lax.dot_general(
        lhs, rhs, (((1,), (1,)), ((), ())), preferred_element_type=jnp.float32
    )

    @pl.when(step == 0)
    def _():
        out_ref[...] = part

    @pl.when(step > 0)
    def _():
        out_ref[...] += part


def drop_source(cells, rates, row_count, slab_width):
    drops = cells.shape[0]
    pieces = []
    rest = rates
    for _ in range(PIECES):
        piece = lax.reduce_precision(rest, exponent_bits=8, mantissa_bits=7)
        pieces.append(piece)
        rest = rest - piece
    pieces = jnp.stack(pieces, axis=1).reshape(2 * PIECES, drops)
    rows = (cells // slab_width).reshape(1, drops)
    cols = (cells % slab_width).reshape(1, drops)
    width = 2 * PIECES * slab_width
    chunk = min(CHUNK, drops)
    summed = pl.pallas_call(
        source_kernel,
        grid=(drops // chunk,),
        in_specs=[
            pl.BlockSpec((1, chunk), lambda i: (0, i)),
            pl.BlockSpec((1, chunk), lambda i: (0, i)),
            pl.BlockSpec((2 * PIECES, chunk), lambda i: (0, i)),
        ],
        out_specs=pl.BlockSpec((row_count, width), lambda i: (0, 0)),
        out_shape=jax.ShapeDtypeStruct((row_count, width), jnp.float32),
        compiler_params=pltpu.CompilerParams(vmem_limit_bytes=48 * 1024 * 1024),
        cost_estimate=pl.CostEstimate(
            flops=2 * row_count * width * drops, transcendentals=0, bytes_accessed=4 * row_count * width
        ),
    )(rows, cols, pieces)
    summed = summed.reshape(row_count, 2, PIECES, slab_width)
    total = summed[:, :, 0]
    for p in range(1, PIECES):
        total = total + summed[:, :, p]
    return jnp.transpose(total, (1, 0, 2))


def per_device(
    field,
    drop_cell,
    drop_plane,
    drop_rate,
    diffusivity,
    wall_eigen,
    basis_part,
    dual_part,
    bulk_shift,
):
    field_count, plane_count, row_count, slab_width = field.shape
    gx_count = lax.axis_size("gx")
    gz_count = lax.axis_size("gz")
    total_cells = slab_width * gx_count
    plane_cells = row_count * slab_width
    rows_here = row_count // gx_count

    plane_here = lax.axis_index("gz")
    packed = jnp.concatenate(
        [(drop_plane * plane_cells + drop_cell).astype(jnp.float32)[None, :], drop_rate], axis=0
    )
    shares = [packed] + [
        lax.ppermute(packed, "gz", [(i, (i + shift) % gz_count) for i in range(gz_count)])
        for shift in range(1, gz_count)
    ]
    packed = jnp.concatenate(shares, axis=1)
    keys = packed[0].astype(jnp.int32)
    cells = keys % plane_cells
    planes = keys // plane_cells
    rates = jnp.where((planes == plane_here)[None, :], packed[1:], 0.0)
    source = drop_source(cells, rates, row_count, slab_width)
    identity = jnp.eye(row_count, dtype=jnp.float32)
    dual_full = identity + dual_part
    calm = jnp.einsum("ay,fyx->fax", dual_full, field[:2, 0], precision=HI)
    calm = lax.all_to_all(calm, "gx", 1, 1, tiled=True)
    fed = jnp.einsum("ay,fyx->fax", dual_full, field[2:, 0] + source, precision=HI)
    fed = lax.all_to_all(fed, "gx", 1, 1, tiled=True)
    spread = jnp.concatenate([calm, fed], axis=0)
    spread = spread.reshape(field_count, gx_count, rows_here, slab_width)

    d_index = jnp.arange(gx_count, dtype=jnp.int32)
    j_index = jnp.arange(slab_width, dtype=jnp.int32)
    c64, s64 = phase(d_index[:, None] * d_index[None, :], gx_count)
    ct, st = phase(d_index[:, None] * j_index[None, :], total_cells)
    c128, s128 = phase(j_index[:, None] * j_index[None, :], slab_width)

    a_real = jnp.einsum("kd,fdaj->fkaj", c64, spread, precision=HI)
    a_imag = -jnp.einsum("kd,fdaj->fkaj", s64, spread, precision=HI)
    ct4 = ct[None, :, None, :]
    st4 = st[None, :, None, :]
    b_real = a_real * ct4 + a_imag * st4
    b_imag = a_imag * ct4 - a_real * st4
    joined = jnp.concatenate([b_real, b_imag], axis=-1)
    forward_table = jnp.concatenate(
        [jnp.concatenate([c128, -s128], axis=1), jnp.concatenate([s128, c128], axis=1)], axis=0
    )
    spec = jnp.einsum("fkaj,jm->fkam", joined, forward_table, precision=HI)
    spec_real = spec[..., :slab_width]
    spec_imag = spec[..., slab_width:]

    mode_index = d_index[:, None] + gx_count * j_index[None, :]
    folded = jnp.minimum(mode_index, total_cells - mode_index).astype(jnp.float32)
    wavenumber = 2.0 * math.pi / total_cells * folded
    position = lax.axis_index("gx")
    eigen_here = lax.dynamic_slice_in_dim(wall_eigen, position * rows_here, rows_here)
    growth = diffusivity[:, None, None, None] * (
        eigen_here[None, None, :, None] + (wavenumber**2)[None, :, None, :]
    )
    damping = (1.0 - growth) / (1.0 + growth)
    signed = jnp.where(2 * mode_index >= total_cells, mode_index - total_cells, mode_index).astype(
        jnp.float32
    )
    travel = 2.0 * math.pi / total_cells * signed * bulk_shift[0]
    cos_travel = jnp.cos(travel)[None, :, None, :]
    sin_travel = jnp.sin(travel)[None, :, None, :]
    factor_real = damping * cos_travel
    factor_imag = -damping * sin_travel
    turned_real = spec_real * factor_real - spec_imag * factor_imag
    turned_imag = spec_real * factor_imag + spec_imag * factor_real

    joined = jnp.concatenate([turned_real, turned_imag], axis=-1)
    inverse_table = jnp.concatenate(
        [jnp.concatenate([c128, s128], axis=1), jnp.concatenate([-s128, c128], axis=1)], axis=0
    )
    back = jnp.einsum("fkam,mj->fkaj", joined, inverse_table, precision=HI)
    back_real = back[..., :slab_width]
    back_imag = back[..., slab_width:]
    e_real = back_real * ct4 - back_imag * st4
    e_imag = back_real * st4 + back_imag * ct4
    filtered = (
        jnp.einsum("dk,fkaj->fdaj", c64, e_real, precision=HI)
        - jnp.einsum("dk,fkaj->fdaj", s64, e_imag, precision=HI)
    ) / total_cells

    filtered = filtered.reshape(field_count, row_count, slab_width)
    gathered = lax.all_to_all(filtered, "gx", 1, 1, tiled=True)
    result = jnp.einsum("ya,fax->fyx", identity + basis_part, gathered, precision=HI)
    return result[:, None]


def solution(mesh):
    in_specs = (
        P(None, "gz", None, "gx"),
        P(("gx", "gz")),
        P(("gx", "gz")),
        P(None, ("gx", "gz")),
        P(),
        P(),
        P(),
        P(),
        P(),
    )
    out_specs = P(None, "gz", None, "gx")
    return jax.shard_map(
        per_device, mesh=mesh, in_specs=in_specs, out_specs=out_specs, check_vma=False
    )
```

```python
import math

import jax
import jax.numpy as jnp
from jax import lax
from jax.experimental import pallas as pl
from jax.experimental.pallas import tpu as pltpu
from jax.sharding import PartitionSpec as P

HI = lax.Precision.HIGH


def phase(numer, length):
    angle = 2.0 * math.pi / length * (numer % length).astype(jnp.float32)
    return jnp.cos(angle), jnp.sin(angle)


PIECES = 2
CHUNK = 2048


def source_kernel(row_ref, col_ref, piece_ref, out_ref):
    step = pl.program_id(0)
    row_count = out_ref.shape[0]
    slab_width = out_ref.shape[1] // piece_ref.shape[0]
    chunk = row_ref.shape[1]
    rows = row_ref[...]
    cols = col_ref[...]
    row_hit = lax.broadcasted_iota(jnp.int32, (row_count, chunk), 0) == rows
    lhs = jnp.where(row_hit, 1.0, 0.0).astype(jnp.bfloat16)
    col_hit = lax.broadcasted_iota(jnp.int32, (slab_width, chunk), 0) == cols
    pieces = piece_ref[...]
    rhs = jnp.concatenate(
        [jnp.where(col_hit, pieces[p : p + 1, :], 0.0) for p in range(pieces.shape[0])], axis=0
    ).astype(jnp.bfloat16)
    part = lax.dot_general(
        lhs, rhs, (((1,), (1,)), ((), ())), preferred_element_type=jnp.float32
    )

    @pl.when(step == 0)
    def _():
        out_ref[...] = part

    @pl.when(step > 0)
    def _():
        out_ref[...] += part


def drop_source(cells, rates, row_count, slab_width):
    drops = cells.shape[0]
    pieces = []
    rest = rates
    for _ in range(PIECES):
        piece = lax.reduce_precision(rest, exponent_bits=8, mantissa_bits=7)
        pieces.append(piece)
        rest = rest - piece
    pieces = jnp.stack(pieces, axis=1).reshape(2 * PIECES, drops)
    rows = (cells // slab_width).reshape(1, drops)
    cols = (cells % slab_width).reshape(1, drops)
    width = 2 * PIECES * slab_width
    chunk = min(CHUNK, drops)
    summed = pl.pallas_call(
        source_kernel,
        grid=(drops // chunk,),
        in_specs=[
            pl.BlockSpec((1, chunk), lambda i: (0, i)),
            pl.BlockSpec((1, chunk), lambda i: (0, i)),
            pl.BlockSpec((2 * PIECES, chunk), lambda i: (0, i)),
        ],
        out_specs=pl.BlockSpec((row_count, width), lambda i: (0, 0)),
        out_shape=jax.ShapeDtypeStruct((row_count, width), jnp.float32),
        compiler_params=pltpu.CompilerParams(vmem_limit_bytes=48 * 1024 * 1024),
        cost_estimate=pl.CostEstimate(
            flops=2 * row_count * width * drops, transcendentals=0, bytes_accessed=4 * row_count * width
        ),
    )(rows, cols, pieces)
    summed = summed.reshape(row_count, 2, PIECES, slab_width)
    total = summed[:, :, 0]
    for p in range(1, PIECES):
        total = total + summed[:, :, p]
    return jnp.transpose(total, (1, 0, 2))


def dft_tables(gx_count, slab_width):
    total_cells = gx_count * slab_width
    d_index = jnp.arange(gx_count, dtype=jnp.int32)
    j_index = jnp.arange(slab_width, dtype=jnp.int32)
    c64, s64 = phase(d_index[:, None] * d_index[None, :], gx_count)
    ct, st = phase(d_index[:, None] * j_index[None, :], total_cells)
    c128, s128 = phase(j_index[:, None] * j_index[None, :], slab_width)
    return d_index, j_index, c64, s64, ct, st, c128, s128


def fft_filter(spread, diffusivity, eigen_here, bulk_shift, tables):
    d_index, j_index, c64, s64, ct, st, c128, s128 = tables
    field_count, row_count, slab_width = spread.shape
    gx_count = c64.shape[0]
    rows_here = row_count // gx_count
    total_cells = gx_count * slab_width
    spread = spread.reshape(field_count, gx_count, rows_here, slab_width)

    a_real = jnp.einsum("kd,fdaj->fkaj", c64, spread, precision=HI)
    a_imag = -jnp.einsum("kd,fdaj->fkaj", s64, spread, precision=HI)
    ct4 = ct[None, :, None, :]
    st4 = st[None, :, None, :]
    b_real = a_real * ct4 + a_imag * st4
    b_imag = a_imag * ct4 - a_real * st4
    joined = jnp.concatenate([b_real, b_imag], axis=-1)
    forward_table = jnp.concatenate(
        [jnp.concatenate([c128, -s128], axis=1), jnp.concatenate([s128, c128], axis=1)], axis=0
    )
    spec = jnp.einsum("fkaj,jm->fkam", joined, forward_table, precision=HI)
    spec_real = spec[..., :slab_width]
    spec_imag = spec[..., slab_width:]

    mode_index = d_index[:, None] + gx_count * j_index[None, :]
    folded = jnp.minimum(mode_index, total_cells - mode_index).astype(jnp.float32)
    wavenumber = 2.0 * math.pi / total_cells * folded
    growth = diffusivity[:, None, None, None] * (
        eigen_here[None, None, :, None] + (wavenumber**2)[None, :, None, :]
    )
    damping = (1.0 - growth) / (1.0 + growth)
    signed = jnp.where(2 * mode_index >= total_cells, mode_index - total_cells, mode_index).astype(
        jnp.float32
    )
    travel = 2.0 * math.pi / total_cells * signed * bulk_shift[0]
    cos_travel = jnp.cos(travel)[None, :, None, :]
    sin_travel = jnp.sin(travel)[None, :, None, :]
    factor_real = damping * cos_travel
    factor_imag = -damping * sin_travel
    turned_real = spec_real * factor_real - spec_imag * factor_imag
    turned_imag = spec_real * factor_imag + spec_imag * factor_real

    joined = jnp.concatenate([turned_real, turned_imag], axis=-1)
    inverse_table = jnp.concatenate(
        [jnp.concatenate([c128, s128], axis=1), jnp.concatenate([-s128, c128], axis=1)], axis=0
    )
    back = jnp.einsum("fkam,mj->fkaj", joined, inverse_table, precision=HI)
    back_real = back[..., :slab_width]
    back_imag = back[..., slab_width:]
    e_real = back_real * ct4 - back_imag * st4
    e_imag = back_real * st4 + back_imag * ct4
    filtered = (
        jnp.einsum("dk,fkaj->fdaj", c64, e_real, precision=HI)
        - jnp.einsum("dk,fkaj->fdaj", s64, e_imag, precision=HI)
    ) / total_cells

    return filtered.reshape(field_count, row_count, slab_width)


def per_device(
    field,
    drop_cell,
    drop_plane,
    drop_rate,
    diffusivity,
    wall_eigen,
    basis_part,
    dual_part,
    bulk_shift,
):
    field_count, plane_count, row_count, slab_width = field.shape
    gx_count = lax.axis_size("gx")
    gz_count = lax.axis_size("gz")
    total_cells = slab_width * gx_count
    plane_cells = row_count * slab_width
    rows_here = row_count // gx_count

    plane_here = lax.axis_index("gz")
    packed = jnp.concatenate(
        [(drop_plane * plane_cells + drop_cell).astype(jnp.float32)[None, :], drop_rate], axis=0
    )
    shares = [packed] + [
        lax.ppermute(packed, "gz", [(i, (i + shift) % gz_count) for i in range(gz_count)])
        for shift in range(1, gz_count)
    ]
    packed = jnp.concatenate(shares, axis=1)
    keys = packed[0].astype(jnp.int32)
    cells = keys % plane_cells
    planes = keys // plane_cells
    rates = jnp.where((planes == plane_here)[None, :], packed[1:], 0.0)
    source = drop_source(cells, rates, row_count, slab_width)
    identity = jnp.eye(row_count, dtype=jnp.float32)
    dual_full = identity + dual_part
    calm = jnp.einsum("ay,fyx->fax", dual_full, field[:2, 0], precision=HI)
    calm = lax.all_to_all(calm, "gx", 1, 1, tiled=True)
    fed = jnp.einsum("ay,fyx->fax", dual_full, field[2:, 0] + source, precision=HI)
    fed = lax.all_to_all(fed, "gx", 1, 1, tiled=True)
    tables = dft_tables(gx_count, slab_width)
    position = lax.axis_index("gx")
    eigen_here = lax.dynamic_slice_in_dim(wall_eigen, position * rows_here, rows_here)
    calm = fft_filter(calm, diffusivity[:2], eigen_here, bulk_shift, tables)
    calm, fed = lax.optimization_barrier((calm, fed))
    fed = fft_filter(fed, diffusivity[2:], eigen_here, bulk_shift, tables)
    filtered = jnp.concatenate([calm, fed], axis=0)
    filtered = filtered.reshape(field_count, row_count, slab_width)
    gathered = lax.all_to_all(filtered, "gx", 1, 1, tiled=True)
    result = jnp.einsum("ya,fax->fyx", identity + basis_part, gathered, precision=HI)
    return result[:, None]


def solution(mesh):
    in_specs = (
        P(None, "gz", None, "gx"),
        P(("gx", "gz")),
        P(("gx", "gz")),
        P(None, ("gx", "gz")),
        P(),
        P(),
        P(),
        P(),
        P(),
    )
    out_specs = P(None, "gz", None, "gx")
    return jax.shard_map(
        per_device, mesh=mesh, in_specs=in_specs, out_specs=out_specs, check_vma=False
    )
```

```python
import math

import jax
import jax.numpy as jnp
from jax import lax
from jax.experimental import pallas as pl
from jax.experimental.pallas import tpu as pltpu
from jax.sharding import PartitionSpec as P

HI = lax.Precision.HIGH
EXACT = lax.Precision.HIGHEST


def phase(numer, length):
    angle = 2.0 * math.pi / length * (numer % length).astype(jnp.float32)
    return jnp.cos(angle), jnp.sin(angle)


PIECES = 2
CHUNK = 2048


def source_kernel(row_ref, col_ref, piece_ref, out_ref):
    step = pl.program_id(0)
    row_count = out_ref.shape[0]
    slab_width = out_ref.shape[1] // piece_ref.shape[0]
    chunk = row_ref.shape[1]
    rows = row_ref[...]
    cols = col_ref[...]
    row_hit = lax.broadcasted_iota(jnp.int32, (row_count, chunk), 0) == rows
    lhs = jnp.where(row_hit, 1.0, 0.0).astype(jnp.bfloat16)
    col_hit = lax.broadcasted_iota(jnp.int32, (slab_width, chunk), 0) == cols
    pieces = piece_ref[...]
    rhs = jnp.concatenate(
        [jnp.where(col_hit, pieces[p : p + 1, :], 0.0) for p in range(pieces.shape[0])], axis=0
    ).astype(jnp.bfloat16)
    part = lax.dot_general(
        lhs, rhs, (((1,), (1,)), ((), ())), preferred_element_type=jnp.float32
    )

    @pl.when(step == 0)
    def _():
        out_ref[...] = part

    @pl.when(step > 0)
    def _():
        out_ref[...] += part


def drop_source(cells, rates, row_count, slab_width):
    drops = cells.shape[0]
    pieces = []
    rest = rates
    for _ in range(PIECES):
        piece = lax.reduce_precision(rest, exponent_bits=8, mantissa_bits=7)
        pieces.append(piece)
        rest = rest - piece
    pieces = jnp.stack(pieces, axis=1).reshape(2 * PIECES, drops)
    rows = (cells // slab_width).reshape(1, drops)
    cols = (cells % slab_width).reshape(1, drops)
    width = 2 * PIECES * slab_width
    chunk = min(CHUNK, drops)
    summed = pl.pallas_call(
        source_kernel,
        grid=(drops // chunk,),
        in_specs=[
            pl.BlockSpec((1, chunk), lambda i: (0, i)),
            pl.BlockSpec((1, chunk), lambda i: (0, i)),
            pl.BlockSpec((2 * PIECES, chunk), lambda i: (0, i)),
        ],
        out_specs=pl.BlockSpec((row_count, width), lambda i: (0, 0)),
        out_shape=jax.ShapeDtypeStruct((row_count, width), jnp.float32),
        compiler_params=pltpu.CompilerParams(vmem_limit_bytes=48 * 1024 * 1024),
        cost_estimate=pl.CostEstimate(
            flops=2 * row_count * width * drops, transcendentals=0, bytes_accessed=4 * row_count * width
        ),
    )(rows, cols, pieces)
    summed = summed.reshape(row_count, 2, PIECES, slab_width)
    total = summed[:, :, 0]
    for p in range(1, PIECES):
        total = total + summed[:, :, p]
    return jnp.transpose(total, (1, 0, 2))


def dft_tables(gx_count, slab_width):
    total_cells = gx_count * slab_width
    d_index = jnp.arange(gx_count, dtype=jnp.int32)
    j_index = jnp.arange(slab_width, dtype=jnp.int32)
    c64, s64 = phase(d_index[:, None] * d_index[None, :], gx_count)
    ct, st = phase(d_index[:, None] * j_index[None, :], total_cells)
    c128, s128 = phase(j_index[:, None] * j_index[None, :], slab_width)
    return d_index, j_index, c64, s64, ct, st, c128, s128


def fft_filter(spread, diffusivity, eigen_here, bulk_shift, tables):
    d_index, j_index, c64, s64, ct, st, c128, s128 = tables
    field_count, row_count, slab_width = spread.shape
    gx_count = c64.shape[0]
    rows_here = row_count // gx_count
    total_cells = gx_count * slab_width
    spread = spread.reshape(field_count, gx_count, rows_here, slab_width)

    a_real = jnp.einsum("kd,fdaj->fkaj", c64, spread, precision=EXACT)
    a_imag = -jnp.einsum("kd,fdaj->fkaj", s64, spread, precision=EXACT)
    ct4 = ct[None, :, None, :]
    st4 = st[None, :, None, :]
    b_real = a_real * ct4 + a_imag * st4
    b_imag = a_imag * ct4 - a_real * st4
    joined = jnp.concatenate([b_real, b_imag], axis=-1)
    forward_table = jnp.concatenate(
        [jnp.concatenate([c128, -s128], axis=1), jnp.concatenate([s128, c128], axis=1)], axis=0
    )
    spec = jnp.einsum("fkaj,jm->fkam", joined, forward_table, precision=EXACT)
    spec_real = spec[..., :slab_width]
    spec_imag = spec[..., slab_width:]

    mode_index = d_index[:, None] + gx_count * j_index[None, :]
    folded = jnp.minimum(mode_index, total_cells - mode_index).astype(jnp.float32)
    wavenumber = 2.0 * math.pi / total_cells * folded
    growth = diffusivity[:, None, None, None] * (
        eigen_here[None, None, :, None] + (wavenumber**2)[None, :, None, :]
    )
    damping = (1.0 - growth) / (1.0 + growth)
    signed = jnp.where(2 * mode_index >= total_cells, mode_index - total_cells, mode_index).astype(
        jnp.float32
    )
    travel = 2.0 * math.pi / total_cells * signed * bulk_shift[0]
    cos_travel = jnp.cos(travel)[None, :, None, :]
    sin_travel = jnp.sin(travel)[None, :, None, :]
    factor_real = damping * cos_travel
    factor_imag = -damping * sin_travel
    turned_real = spec_real * factor_real - spec_imag * factor_imag
    turned_imag = spec_real * factor_imag + spec_imag * factor_real

    joined = jnp.concatenate([turned_real, turned_imag], axis=-1)
    inverse_table = jnp.concatenate(
        [jnp.concatenate([c128, s128], axis=1), jnp.concatenate([-s128, c128], axis=1)], axis=0
    )
    back = jnp.einsum("fkam,mj->fkaj", joined, inverse_table, precision=EXACT)
    back_real = back[..., :slab_width]
    back_imag = back[..., slab_width:]
    e_real = back_real * ct4 - back_imag * st4
    e_imag = back_real * st4 + back_imag * ct4
    filtered = (
        jnp.einsum("dk,fkaj->fdaj", c64, e_real, precision=EXACT)
        - jnp.einsum("dk,fkaj->fdaj", s64, e_imag, precision=EXACT)
    ) / total_cells

    return filtered.reshape(field_count, row_count, slab_width)


def per_device(
    field,
    drop_cell,
    drop_plane,
    drop_rate,
    diffusivity,
    wall_eigen,
    basis_part,
    dual_part,
    bulk_shift,
):
    field_count, plane_count, row_count, slab_width = field.shape
    gx_count = lax.axis_size("gx")
    gz_count = lax.axis_size("gz")
    total_cells = slab_width * gx_count
    plane_cells = row_count * slab_width
    rows_here = row_count // gx_count

    plane_here = lax.axis_index("gz")
    packed = jnp.concatenate(
        [(drop_plane * plane_cells + drop_cell).astype(jnp.float32)[None, :], drop_rate], axis=0
    )
    shares = [packed] + [
        lax.ppermute(packed, "gz", [(i, (i + shift) % gz_count) for i in range(gz_count)])
        for shift in range(1, gz_count)
    ]
    packed = jnp.concatenate(shares, axis=1)
    keys = packed[0].astype(jnp.int32)
    cells = keys % plane_cells
    planes = keys // plane_cells
    rates = jnp.where((planes == plane_here)[None, :], packed[1:], 0.0)
    source = drop_source(cells, rates, row_count, slab_width)
    identity = jnp.eye(row_count, dtype=jnp.float32)
    dual_full = identity + dual_part
    calm = jnp.einsum("ay,fyx->fax", dual_full, field[:2, 0], precision=HI)
    calm = lax.all_to_all(calm, "gx", 1, 1, tiled=True)
    fed = jnp.einsum("ay,fyx->fax", dual_full, field[2:, 0] + source, precision=HI)
    fed = lax.all_to_all(fed, "gx", 1, 1, tiled=True)
    tables = dft_tables(gx_count, slab_width)
    position = lax.axis_index("gx")
    eigen_here = lax.dynamic_slice_in_dim(wall_eigen, position * rows_here, rows_here)
    calm = fft_filter(calm, diffusivity[:2], eigen_here, bulk_shift, tables)
    calm, fed = lax.optimization_barrier((calm, fed))
    fed = fft_filter(fed, diffusivity[2:], eigen_here, bulk_shift, tables)
    filtered = jnp.concatenate([calm, fed], axis=0)
    filtered = filtered.reshape(field_count, row_count, slab_width)
    gathered = lax.all_to_all(filtered, "gx", 1, 1, tiled=True)
    result = jnp.einsum("ya,fax->fyx", identity + basis_part, gathered, precision=HI)
    return result[:, None]


def solution(mesh):
    in_specs = (
        P(None, "gz", None, "gx"),
        P(("gx", "gz")),
        P(("gx", "gz")),
        P(None, ("gx", "gz")),
        P(),
        P(),
        P(),
        P(),
        P(),
    )
    out_specs = P(None, "gz", None, "gx")
    return jax.shard_map(
        per_device, mesh=mesh, in_specs=in_specs, out_specs=out_specs, check_vma=False
    )
```

```python
import math

import jax
import jax.numpy as jnp
from jax import lax
from jax.experimental import pallas as pl
from jax.experimental.pallas import tpu as pltpu
from jax.sharding import PartitionSpec as P

HI = lax.Precision.HIGH
EXACT = lax.Precision.HIGHEST


def phase(numer, length):
    angle = 2.0 * math.pi / length * (numer % length).astype(jnp.float32)
    return jnp.cos(angle), jnp.sin(angle)


PIECES = 2
CHUNK = 2048


def source_kernel(row_ref, col_ref, piece_ref, out_ref):
    step = pl.program_id(0)
    row_count = out_ref.shape[0]
    slab_width = out_ref.shape[1] // piece_ref.shape[0]
    chunk = row_ref.shape[1]
    rows = row_ref[...]
    cols = col_ref[...]
    row_hit = lax.broadcasted_iota(jnp.int32, (row_count, chunk), 0) == rows
    lhs = jnp.where(row_hit, 1.0, 0.0).astype(jnp.bfloat16)
    col_hit = lax.broadcasted_iota(jnp.int32, (slab_width, chunk), 0) == cols
    pieces = piece_ref[...]
    rhs = jnp.concatenate(
        [jnp.where(col_hit, pieces[p : p + 1, :], 0.0) for p in range(pieces.shape[0])], axis=0
    ).astype(jnp.bfloat16)
    part = lax.dot_general(
        lhs, rhs, (((1,), (1,)), ((), ())), preferred_element_type=jnp.float32
    )

    @pl.when(step == 0)
    def _():
        out_ref[...] = part

    @pl.when(step > 0)
    def _():
        out_ref[...] += part


def drop_source(cells, rates, row_count, slab_width):
    drops = cells.shape[0]
    pieces = []
    rest = rates
    for _ in range(PIECES):
        piece = lax.reduce_precision(rest, exponent_bits=8, mantissa_bits=7)
        pieces.append(piece)
        rest = rest - piece
    pieces = jnp.stack(pieces, axis=1).reshape(2 * PIECES, drops)
    rows = (cells // slab_width).reshape(1, drops)
    cols = (cells % slab_width).reshape(1, drops)
    width = 2 * PIECES * slab_width
    chunk = min(CHUNK, drops)
    summed = pl.pallas_call(
        source_kernel,
        grid=(drops // chunk,),
        in_specs=[
            pl.BlockSpec((1, chunk), lambda i: (0, i)),
            pl.BlockSpec((1, chunk), lambda i: (0, i)),
            pl.BlockSpec((2 * PIECES, chunk), lambda i: (0, i)),
        ],
        out_specs=pl.BlockSpec((row_count, width), lambda i: (0, 0)),
        out_shape=jax.ShapeDtypeStruct((row_count, width), jnp.float32),
        compiler_params=pltpu.CompilerParams(vmem_limit_bytes=48 * 1024 * 1024),
        cost_estimate=pl.CostEstimate(
            flops=2 * row_count * width * drops, transcendentals=0, bytes_accessed=4 * row_count * width
        ),
    )(rows, cols, pieces)
    summed = summed.reshape(row_count, 2, PIECES, slab_width)
    total = summed[:, :, 0]
    for p in range(1, PIECES):
        total = total + summed[:, :, p]
    return jnp.transpose(total, (1, 0, 2))


def dft_tables(gx_count, slab_width):
    total_cells = gx_count * slab_width
    d_index = jnp.arange(gx_count, dtype=jnp.int32)
    j_index = jnp.arange(slab_width, dtype=jnp.int32)
    c64, s64 = phase(d_index[:, None] * d_index[None, :], gx_count)
    ct, st = phase(d_index[:, None] * j_index[None, :], total_cells)
    c128, s128 = phase(j_index[:, None] * j_index[None, :], slab_width)
    return d_index, j_index, c64, s64, ct, st, c128, s128


def fft_filter(spread, diffusivity, eigen_here, bulk_shift, tables):
    d_index, j_index, c64, s64, ct, st, c128, s128 = tables
    field_count, row_count, slab_width = spread.shape
    gx_count = c64.shape[0]
    rows_here = row_count // gx_count
    total_cells = gx_count * slab_width
    spread = spread.reshape(field_count, gx_count, rows_here, slab_width)

    a_real = jnp.einsum("kd,fdaj->fkaj", c64, spread, precision=EXACT)
    a_imag = -jnp.einsum("kd,fdaj->fkaj", s64, spread, precision=EXACT)
    ct4 = ct[None, :, None, :]
    st4 = st[None, :, None, :]
    b_real = a_real * ct4 + a_imag * st4
    b_imag = a_imag * ct4 - a_real * st4
    joined = jnp.concatenate([b_real, b_imag], axis=-1)
    forward_table = jnp.concatenate(
        [jnp.concatenate([c128, -s128], axis=1), jnp.concatenate([s128, c128], axis=1)], axis=0
    )
    spec = jnp.einsum("fkaj,jm->fkam", joined, forward_table, precision=EXACT)
    spec_real = spec[..., :slab_width]
    spec_imag = spec[..., slab_width:]

    mode_index = d_index[:, None] + gx_count * j_index[None, :]
    folded = jnp.minimum(mode_index, total_cells - mode_index).astype(jnp.float32)
    wavenumber = 2.0 * math.pi / total_cells * folded
    growth = diffusivity[:, None, None, None] * (
        eigen_here[None, None, :, None] + (wavenumber**2)[None, :, None, :]
    )
    damping = (1.0 - growth) / (1.0 + growth)
    signed = jnp.where(2 * mode_index >= total_cells, mode_index - total_cells, mode_index).astype(
        jnp.float32
    )
    travel = 2.0 * math.pi / total_cells * signed * bulk_shift[0]
    cos_travel = jnp.cos(travel)[None, :, None, :]
    sin_travel = jnp.sin(travel)[None, :, None, :]
    factor_real = damping * cos_travel
    factor_imag = -damping * sin_travel
    turned_real = spec_real * factor_real - spec_imag * factor_imag
    turned_imag = spec_real * factor_imag + spec_imag * factor_real

    joined = jnp.concatenate([turned_real, turned_imag], axis=-1)
    inverse_table = jnp.concatenate(
        [jnp.concatenate([c128, s128], axis=1), jnp.concatenate([-s128, c128], axis=1)], axis=0
    )
    back = jnp.einsum("fkam,mj->fkaj", joined, inverse_table, precision=EXACT)
    back_real = back[..., :slab_width]
    back_imag = back[..., slab_width:]
    e_real = back_real * ct4 - back_imag * st4
    e_imag = back_real * st4 + back_imag * ct4
    filtered = (
        jnp.einsum("dk,fkaj->fdaj", c64, e_real, precision=EXACT)
        - jnp.einsum("dk,fkaj->fdaj", s64, e_imag, precision=EXACT)
    ) / total_cells

    return filtered.reshape(field_count, row_count, slab_width)


def per_device(
    field,
    drop_cell,
    drop_plane,
    drop_rate,
    diffusivity,
    wall_eigen,
    basis_part,
    dual_part,
    bulk_shift,
):
    field_count, plane_count, row_count, slab_width = field.shape
    gx_count = lax.axis_size("gx")
    gz_count = lax.axis_size("gz")
    total_cells = slab_width * gx_count
    plane_cells = row_count * slab_width
    rows_here = row_count // gx_count

    plane_here = lax.axis_index("gz")
    packed = jnp.concatenate(
        [(drop_plane * plane_cells + drop_cell).astype(jnp.float32)[None, :], drop_rate], axis=0
    )
    shares = [packed] + [
        lax.ppermute(packed, "gz", [(i, (i + shift) % gz_count) for i in range(gz_count)])
        for shift in range(1, gz_count)
    ]
    packed = jnp.concatenate(shares, axis=1)
    keys = packed[0].astype(jnp.int32)
    cells = keys % plane_cells
    planes = keys // plane_cells
    rates = jnp.where((planes == plane_here)[None, :], packed[1:], 0.0)
    source = drop_source(cells, rates, row_count, slab_width)
    identity = jnp.eye(row_count, dtype=jnp.float32)
    dual_full = identity + dual_part
    calm = jnp.einsum("ay,fyx->fax", dual_full, field[:2, 0], precision=HI)
    calm = lax.all_to_all(calm, "gx", 1, 1, tiled=True)
    fed = jnp.einsum("ay,fyx->fax", dual_full, field[2:, 0] + source, precision=HI)
    fed = lax.all_to_all(fed, "gx", 1, 1, tiled=True)
    tables = dft_tables(gx_count, slab_width)
    position = lax.axis_index("gx")
    eigen_here = lax.dynamic_slice_in_dim(wall_eigen, position * rows_here, rows_here)
    calm = fft_filter(calm, diffusivity[:2], eigen_here, bulk_shift, tables)
    calm, fed = lax.optimization_barrier((calm, fed))
    calm = lax.all_to_all(calm, "gx", 1, 1, tiled=True)
    fed = fft_filter(fed, diffusivity[2:], eigen_here, bulk_shift, tables)
    fed = lax.all_to_all(fed, "gx", 1, 1, tiled=True)
    basis_full = identity + basis_part
    result = jnp.concatenate(
        [
            jnp.einsum("ya,fax->fyx", basis_full, calm, precision=HI),
            jnp.einsum("ya,fax->fyx", basis_full, fed, precision=HI),
        ],
        axis=0,
    )
    return result[:, None]


def solution(mesh):
    in_specs = (
        P(None, "gz", None, "gx"),
        P(("gx", "gz")),
        P(("gx", "gz")),
        P(None, ("gx", "gz")),
        P(),
        P(),
        P(),
        P(),
        P(),
    )
    out_specs = P(None, "gz", None, "gx")
    return jax.shard_map(
        per_device, mesh=mesh, in_specs=in_specs, out_specs=out_specs, check_vma=False
    )
```

```python
import math

import jax
import jax.numpy as jnp
from jax import lax
from jax.experimental import pallas as pl
from jax.experimental.pallas import tpu as pltpu
from jax.sharding import PartitionSpec as P

HI = lax.Precision.HIGH
EXACT = lax.Precision.HIGHEST


def phase(numer, length):
    angle = 2.0 * math.pi / length * (numer % length).astype(jnp.float32)
    return jnp.cos(angle), jnp.sin(angle)


PIECES = 2
CHUNK = 2048


def source_kernel(row_ref, col_ref, piece_ref, field_ref, out_ref, acc_ref):
    step = pl.program_id(0)
    row_count = acc_ref.shape[0]
    slab_width = out_ref.shape[2]
    chunk = row_ref.shape[1]
    rows = row_ref[...]
    cols = col_ref[...]
    row_hit = lax.broadcasted_iota(jnp.int32, (row_count, chunk), 0) == rows
    lhs = jnp.where(row_hit, 1.0, 0.0).astype(jnp.bfloat16)
    col_hit = lax.broadcasted_iota(jnp.int32, (slab_width, chunk), 0) == cols
    pieces = piece_ref[...]
    rhs = jnp.concatenate(
        [jnp.where(col_hit, pieces[p : p + 1, :], 0.0) for p in range(pieces.shape[0])], axis=0
    ).astype(jnp.bfloat16)
    part = lax.dot_general(
        lhs, rhs, (((1,), (1,)), ((), ())), preferred_element_type=jnp.float32
    )

    @pl.when(step == 0)
    def _():
        acc_ref[...] = part

    @pl.when(step > 0)
    def _():
        acc_ref[...] += part

    @pl.when(step == pl.num_programs(0) - 1)
    def _():
        for c in range(out_ref.shape[0]):
            total = field_ref[c, 0]
            for p in range(PIECES):
                start = (c * PIECES + p) * slab_width
                total = total + acc_ref[:, start : start + slab_width]
            out_ref[c] = total


def drop_source(cells, rates, field):
    drops = cells.shape[0]
    field_count, _, row_count, slab_width = field.shape
    pieces = []
    rest = rates
    for _ in range(PIECES):
        piece = lax.reduce_precision(rest, exponent_bits=8, mantissa_bits=7)
        pieces.append(piece)
        rest = rest - piece
    pieces = jnp.stack(pieces, axis=1).reshape(2 * PIECES, drops)
    rows = (cells // slab_width).reshape(1, drops)
    cols = (cells % slab_width).reshape(1, drops)
    width = 2 * PIECES * slab_width
    chunk = min(CHUNK, drops)
    return pl.pallas_call(
        source_kernel,
        grid=(drops // chunk,),
        in_specs=[
            pl.BlockSpec((1, chunk), lambda i: (0, i)),
            pl.BlockSpec((1, chunk), lambda i: (0, i)),
            pl.BlockSpec((2 * PIECES, chunk), lambda i: (0, i)),
            pl.BlockSpec((2, 1, row_count, slab_width), lambda i: (1, 0, 0, 0)),
        ],
        out_specs=pl.BlockSpec((2, row_count, slab_width), lambda i: (0, 0, 0)),
        out_shape=jax.ShapeDtypeStruct((2, row_count, slab_width), jnp.float32),
        scratch_shapes=[pltpu.VMEM((row_count, width), jnp.float32)],
        compiler_params=pltpu.CompilerParams(vmem_limit_bytes=48 * 1024 * 1024),
        cost_estimate=pl.CostEstimate(
            flops=2 * row_count * width * drops, transcendentals=0, bytes_accessed=4 * row_count * width
        ),
    )(rows, cols, pieces, field)


def dft_tables(gx_count, slab_width):
    total_cells = gx_count * slab_width
    d_index = jnp.arange(gx_count, dtype=jnp.int32)
    j_index = jnp.arange(slab_width, dtype=jnp.int32)
    c64, s64 = phase(d_index[:, None] * d_index[None, :], gx_count)
    ct, st = phase(d_index[:, None] * j_index[None, :], total_cells)
    c128, s128 = phase(j_index[:, None] * j_index[None, :], slab_width)
    return d_index, j_index, c64, s64, ct, st, c128, s128


def fft_filter(spread, diffusivity, eigen_here, bulk_shift, tables):
    d_index, j_index, c64, s64, ct, st, c128, s128 = tables
    field_count, row_count, slab_width = spread.shape
    gx_count = c64.shape[0]
    rows_here = row_count // gx_count
    total_cells = gx_count * slab_width
    spread = spread.reshape(field_count, gx_count, rows_here, slab_width)

    a_real = jnp.einsum("kd,fdaj->fkaj", c64, spread, precision=EXACT)
    a_imag = -jnp.einsum("kd,fdaj->fkaj", s64, spread, precision=EXACT)
    ct4 = ct[None, :, None, :]
    st4 = st[None, :, None, :]
    b_real = a_real * ct4 + a_imag * st4
    b_imag = a_imag * ct4 - a_real * st4
    joined = jnp.concatenate([b_real, b_imag], axis=-1)
    forward_table = jnp.concatenate(
        [jnp.concatenate([c128, -s128], axis=1), jnp.concatenate([s128, c128], axis=1)], axis=0
    )
    spec = jnp.einsum("fkaj,jm->fkam", joined, forward_table, precision=EXACT)
    spec_real = spec[..., :slab_width]
    spec_imag = spec[..., slab_width:]

    mode_index = d_index[:, None] + gx_count * j_index[None, :]
    folded = jnp.minimum(mode_index, total_cells - mode_index).astype(jnp.float32)
    wavenumber = 2.0 * math.pi / total_cells * folded
    growth = diffusivity[:, None, None, None] * (
        eigen_here[None, None, :, None] + (wavenumber**2)[None, :, None, :]
    )
    damping = (1.0 - growth) / (1.0 + growth)
    signed = jnp.where(2 * mode_index >= total_cells, mode_index - total_cells, mode_index).astype(
        jnp.float32
    )
    travel = 2.0 * math.pi / total_cells * signed * bulk_shift[0]
    cos_travel = jnp.cos(travel)[None, :, None, :]
    sin_travel = jnp.sin(travel)[None, :, None, :]
    factor_real = damping * cos_travel
    factor_imag = -damping * sin_travel
    turned_real = spec_real * factor_real - spec_imag * factor_imag
    turned_imag = spec_real * factor_imag + spec_imag * factor_real

    joined = jnp.concatenate([turned_real, turned_imag], axis=-1)
    inverse_table = jnp.concatenate(
        [jnp.concatenate([c128, s128], axis=1), jnp.concatenate([-s128, c128], axis=1)], axis=0
    )
    back = jnp.einsum("fkam,mj->fkaj", joined, inverse_table, precision=EXACT)
    back_real = back[..., :slab_width]
    back_imag = back[..., slab_width:]
    e_real = back_real * ct4 - back_imag * st4
    e_imag = back_real * st4 + back_imag * ct4
    filtered = (
        jnp.einsum("dk,fkaj->fdaj", c64, e_real, precision=EXACT)
        - jnp.einsum("dk,fkaj->fdaj", s64, e_imag, precision=EXACT)
    ) / total_cells

    return filtered.reshape(field_count, row_count, slab_width)


def per_device(
    field,
    drop_cell,
    drop_plane,
    drop_rate,
    diffusivity,
    wall_eigen,
    basis_part,
    dual_part,
    bulk_shift,
):
    field_count, plane_count, row_count, slab_width = field.shape
    gx_count = lax.axis_size("gx")
    gz_count = lax.axis_size("gz")
    total_cells = slab_width * gx_count
    plane_cells = row_count * slab_width
    rows_here = row_count // gx_count

    plane_here = lax.axis_index("gz")
    packed = jnp.concatenate(
        [(drop_plane * plane_cells + drop_cell).astype(jnp.float32)[None, :], drop_rate], axis=0
    )
    shares = [packed] + [
        lax.ppermute(packed, "gz", [(i, (i + shift) % gz_count) for i in range(gz_count)])
        for shift in range(1, gz_count)
    ]
    packed = jnp.concatenate(shares, axis=1)
    keys = packed[0].astype(jnp.int32)
    cells = keys % plane_cells
    planes = keys // plane_cells
    rates = jnp.where((planes == plane_here)[None, :], packed[1:], 0.0)
    fed_side = drop_source(cells, rates, field)
    identity = jnp.eye(row_count, dtype=jnp.float32)
    dual_full = identity + dual_part
    calm = jnp.einsum("ay,fyx->fax", dual_full, field[:2, 0], precision=HI)
    calm = lax.all_to_all(calm, "gx", 1, 1, tiled=True)
    fed = jnp.einsum("ay,fyx->fax", dual_full, fed_side, precision=HI)
    fed = lax.all_to_all(fed, "gx", 1, 1, tiled=True)
    tables = dft_tables(gx_count, slab_width)
    position = lax.axis_index("gx")
    eigen_here = lax.dynamic_slice_in_dim(wall_eigen, position * rows_here, rows_here)
    calm = fft_filter(calm, diffusivity[:2], eigen_here, bulk_shift, tables)
    calm, fed = lax.optimization_barrier((calm, fed))
    fed = fft_filter(fed, diffusivity[2:], eigen_here, bulk_shift, tables)
    filtered = jnp.concatenate([calm, fed], axis=0)
    filtered = filtered.reshape(field_count, row_count, slab_width)
    gathered = lax.all_to_all(filtered, "gx", 1, 1, tiled=True)
    result = jnp.einsum("ya,fax->fyx", identity + basis_part, gathered, precision=HI)
    return result[:, None]


def solution(mesh):
    in_specs = (
        P(None, "gz", None, "gx"),
        P(("gx", "gz")),
        P(("gx", "gz")),
        P(None, ("gx", "gz")),
        P(),
        P(),
        P(),
        P(),
        P(),
    )
    out_specs = P(None, "gz", None, "gx")
    return jax.shard_map(
        per_device, mesh=mesh, in_specs=in_specs, out_specs=out_specs, check_vma=False
    )
```

```python
import math

import jax
import jax.numpy as jnp
from jax import lax
from jax.experimental import pallas as pl
from jax.experimental.pallas import tpu as pltpu
from jax.sharding import PartitionSpec as P

HI = lax.Precision.HIGH
EXACT = lax.Precision.HIGHEST


def phase(numer, length):
    angle = 2.0 * math.pi / length * (numer % length).astype(jnp.float32)
    return jnp.cos(angle), jnp.sin(angle)


PIECES = 2
CHUNK = 16384


def source_kernel(row_ref, col_ref, piece_ref, field_ref, out_ref, acc_ref):
    step = pl.program_id(0)
    row_count = acc_ref.shape[0]
    slab_width = out_ref.shape[2]
    chunk = row_ref.shape[1]
    rows = row_ref[...]
    cols = col_ref[...]
    row_hit = lax.broadcasted_iota(jnp.int32, (row_count, chunk), 0) == rows
    lhs = jnp.where(row_hit, 1.0, 0.0).astype(jnp.bfloat16)
    col_hit = lax.broadcasted_iota(jnp.int32, (slab_width, chunk), 0) == cols
    pieces = piece_ref[...]
    rhs = jnp.concatenate(
        [jnp.where(col_hit, pieces[p : p + 1, :], 0.0) for p in range(pieces.shape[0])], axis=0
    ).astype(jnp.bfloat16)
    part = lax.dot_general(
        lhs, rhs, (((1,), (1,)), ((), ())), preferred_element_type=jnp.float32
    )

    @pl.when(step == 0)
    def _():
        acc_ref[...] = part

    @pl.when(step > 0)
    def _():
        acc_ref[...] += part

    @pl.when(step == pl.num_programs(0) - 1)
    def _():
        for c in range(out_ref.shape[0]):
            total = field_ref[c, 0]
            for p in range(PIECES):
                start = (c * PIECES + p) * slab_width
                total = total + acc_ref[:, start : start + slab_width]
            out_ref[c] = total


def drop_source(cells, rates, field):
    drops = cells.shape[0]
    field_count, _, row_count, slab_width = field.shape
    pieces = []
    rest = rates
    for _ in range(PIECES):
        piece = lax.reduce_precision(rest, exponent_bits=8, mantissa_bits=7)
        pieces.append(piece)
        rest = rest - piece
    pieces = jnp.stack(pieces, axis=1).reshape(2 * PIECES, drops)
    rows = (cells // slab_width).reshape(1, drops)
    cols = (cells % slab_width).reshape(1, drops)
    width = 2 * PIECES * slab_width
    chunk = min(CHUNK, drops)
    return pl.pallas_call(
        source_kernel,
        grid=(drops // chunk,),
        in_specs=[
            pl.BlockSpec((1, chunk), lambda i: (0, i)),
            pl.BlockSpec((1, chunk), lambda i: (0, i)),
            pl.BlockSpec((2 * PIECES, chunk), lambda i: (0, i)),
            pl.BlockSpec((2, 1, row_count, slab_width), lambda i: (1, 0, 0, 0)),
        ],
        out_specs=pl.BlockSpec((2, row_count, slab_width), lambda i: (0, 0, 0)),
        out_shape=jax.ShapeDtypeStruct((2, row_count, slab_width), jnp.float32),
        scratch_shapes=[pltpu.VMEM((row_count, width), jnp.float32)],
        compiler_params=pltpu.CompilerParams(vmem_limit_bytes=48 * 1024 * 1024),
        cost_estimate=pl.CostEstimate(
            flops=2 * row_count * width * drops, transcendentals=0, bytes_accessed=4 * row_count * width
        ),
    )(rows, cols, pieces, field)


def dft_tables(gx_count, slab_width):
    total_cells = gx_count * slab_width
    d_index = jnp.arange(gx_count, dtype=jnp.int32)
    j_index = jnp.arange(slab_width, dtype=jnp.int32)
    c64, s64 = phase(d_index[:, None] * d_index[None, :], gx_count)
    ct, st = phase(d_index[:, None] * j_index[None, :], total_cells)
    c128, s128 = phase(j_index[:, None] * j_index[None, :], slab_width)
    return d_index, j_index, c64, s64, ct, st, c128, s128


def fft_filter(spread, diffusivity, eigen_here, bulk_shift, tables):
    d_index, j_index, c64, s64, ct, st, c128, s128 = tables
    field_count, row_count, slab_width = spread.shape
    gx_count = c64.shape[0]
    rows_here = row_count // gx_count
    total_cells = gx_count * slab_width
    spread = spread.reshape(field_count, gx_count, rows_here, slab_width)

    a_real = jnp.einsum("kd,fdaj->fkaj", c64, spread, precision=EXACT)
    a_imag = -jnp.einsum("kd,fdaj->fkaj", s64, spread, precision=EXACT)
    ct4 = ct[None, :, None, :]
    st4 = st[None, :, None, :]
    b_real = a_real * ct4 + a_imag * st4
    b_imag = a_imag * ct4 - a_real * st4
    joined = jnp.concatenate([b_real, b_imag], axis=-1)
    forward_table = jnp.concatenate(
        [jnp.concatenate([c128, -s128], axis=1), jnp.concatenate([s128, c128], axis=1)], axis=0
    )
    spec = jnp.einsum("fkaj,jm->fkam", joined, forward_table, precision=EXACT)
    spec_real = spec[..., :slab_width]
    spec_imag = spec[..., slab_width:]

    mode_index = d_index[:, None] + gx_count * j_index[None, :]
    folded = jnp.minimum(mode_index, total_cells - mode_index).astype(jnp.float32)
    wavenumber = 2.0 * math.pi / total_cells * folded
    growth = diffusivity[:, None, None, None] * (
        eigen_here[None, None, :, None] + (wavenumber**2)[None, :, None, :]
    )
    damping = (1.0 - growth) / (1.0 + growth)
    signed = jnp.where(2 * mode_index >= total_cells, mode_index - total_cells, mode_index).astype(
        jnp.float32
    )
    travel = 2.0 * math.pi / total_cells * signed * bulk_shift[0]
    cos_travel = jnp.cos(travel)[None, :, None, :]
    sin_travel = jnp.sin(travel)[None, :, None, :]
    factor_real = damping * cos_travel
    factor_imag = -damping * sin_travel
    turned_real = spec_real * factor_real - spec_imag * factor_imag
    turned_imag = spec_real * factor_imag + spec_imag * factor_real

    joined = jnp.concatenate([turned_real, turned_imag], axis=-1)
    inverse_table = jnp.concatenate(
        [jnp.concatenate([c128, s128], axis=1), jnp.concatenate([-s128, c128], axis=1)], axis=0
    )
    back = jnp.einsum("fkam,mj->fkaj", joined, inverse_table, precision=EXACT)
    back_real = back[..., :slab_width]
    back_imag = back[..., slab_width:]
    e_real = back_real * ct4 - back_imag * st4
    e_imag = back_real * st4 + back_imag * ct4
    filtered = (
        jnp.einsum("dk,fkaj->fdaj", c64, e_real, precision=EXACT)
        - jnp.einsum("dk,fkaj->fdaj", s64, e_imag, precision=EXACT)
    ) / total_cells

    return filtered.reshape(field_count, row_count, slab_width)


def per_device(
    field,
    drop_cell,
    drop_plane,
    drop_rate,
    diffusivity,
    wall_eigen,
    basis_part,
    dual_part,
    bulk_shift,
):
    field_count, plane_count, row_count, slab_width = field.shape
    gx_count = lax.axis_size("gx")
    gz_count = lax.axis_size("gz")
    total_cells = slab_width * gx_count
    plane_cells = row_count * slab_width
    rows_here = row_count // gx_count

    plane_here = lax.axis_index("gz")
    packed = jnp.concatenate(
        [(drop_plane * plane_cells + drop_cell).astype(jnp.float32)[None, :], drop_rate], axis=0
    )
    shares = [packed] + [
        lax.ppermute(packed, "gz", [(i, (i + shift) % gz_count) for i in range(gz_count)])
        for shift in range(1, gz_count)
    ]
    packed = jnp.concatenate(shares, axis=1)
    keys = packed[0].astype(jnp.int32)
    cells = keys % plane_cells
    planes = keys // plane_cells
    rates = jnp.where((planes == plane_here)[None, :], packed[1:], 0.0)
    fed_side = drop_source(cells, rates, field)
    identity = jnp.eye(row_count, dtype=jnp.float32)
    dual_full = identity + dual_part
    calm = jnp.einsum("ay,fyx->fax", dual_full, field[:2, 0], precision=HI)
    calm = lax.all_to_all(calm, "gx", 1, 1, tiled=True)
    fed = jnp.einsum("ay,fyx->fax", dual_full, fed_side, precision=HI)
    fed = lax.all_to_all(fed, "gx", 1, 1, tiled=True)
    tables = dft_tables(gx_count, slab_width)
    position = lax.axis_index("gx")
    eigen_here = lax.dynamic_slice_in_dim(wall_eigen, position * rows_here, rows_here)
    calm = fft_filter(calm, diffusivity[:2], eigen_here, bulk_shift, tables)
    calm, fed = lax.optimization_barrier((calm, fed))
    fed = fft_filter(fed, diffusivity[2:], eigen_here, bulk_shift, tables)
    filtered = jnp.concatenate([calm, fed], axis=0)
    filtered = filtered.reshape(field_count, row_count, slab_width)
    gathered = lax.all_to_all(filtered, "gx", 1, 1, tiled=True)
    result = jnp.einsum("ya,fax->fyx", identity + basis_part, gathered, precision=HI)
    return result[:, None]


def solution(mesh):
    in_specs = (
        P(None, "gz", None, "gx"),
        P(("gx", "gz")),
        P(("gx", "gz")),
        P(None, ("gx", "gz")),
        P(),
        P(),
        P(),
        P(),
        P(),
    )
    out_specs = P(None, "gz", None, "gx")
    return jax.shard_map(
        per_device, mesh=mesh, in_specs=in_specs, out_specs=out_specs, check_vma=False
    )
```

```python
import math

import jax
import jax.numpy as jnp
from jax import lax
from jax.experimental import pallas as pl
from jax.experimental.pallas import tpu as pltpu
from jax.sharding import PartitionSpec as P

HI = lax.Precision.HIGH
EXACT = lax.Precision.HIGHEST


def phase(numer, length):
    angle = 2.0 * math.pi / length * (numer % length).astype(jnp.float32)
    return jnp.cos(angle), jnp.sin(angle)


PIECES = 2
CHUNK = 16384


def source_kernel(row_ref, col_ref, piece_ref, field_ref, out_ref, acc_ref):
    step = pl.program_id(0)
    row_count = acc_ref.shape[0]
    slab_width = out_ref.shape[2]
    chunk = row_ref.shape[1]
    rows = row_ref[...]
    cols = col_ref[...]
    row_hit = lax.broadcasted_iota(jnp.int32, (row_count, chunk), 0) == rows
    lhs = jnp.where(row_hit, 1.0, 0.0).astype(jnp.bfloat16)
    col_hit = lax.broadcasted_iota(jnp.int32, (slab_width, chunk), 0) == cols
    pieces = piece_ref[...]
    rhs = jnp.concatenate(
        [jnp.where(col_hit, pieces[p : p + 1, :], 0.0) for p in range(pieces.shape[0])], axis=0
    ).astype(jnp.bfloat16)
    part = lax.dot_general(
        lhs, rhs, (((1,), (1,)), ((), ())), preferred_element_type=jnp.float32
    )

    @pl.when(step == 0)
    def _():
        acc_ref[...] = part

    @pl.when(step > 0)
    def _():
        acc_ref[...] += part

    @pl.when(step == pl.num_programs(0) - 1)
    def _():
        for c in range(out_ref.shape[0]):
            total = field_ref[c, 0]
            for p in range(PIECES):
                start = (c * PIECES + p) * slab_width
                total = total + acc_ref[:, start : start + slab_width]
            out_ref[c] = total


def drop_source(cells, rates, field):
    drops = cells.shape[0]
    field_count, _, row_count, slab_width = field.shape
    pieces = []
    rest = rates
    for _ in range(PIECES):
        piece = lax.reduce_precision(rest, exponent_bits=8, mantissa_bits=7)
        pieces.append(piece)
        rest = rest - piece
    pieces = jnp.stack(pieces, axis=1).reshape(2 * PIECES, drops)
    rows = (cells // slab_width).reshape(1, drops)
    cols = (cells % slab_width).reshape(1, drops)
    width = 2 * PIECES * slab_width
    chunk = min(CHUNK, drops)
    return pl.pallas_call(
        source_kernel,
        grid=(drops // chunk,),
        in_specs=[
            pl.BlockSpec((1, chunk), lambda i: (0, i)),
            pl.BlockSpec((1, chunk), lambda i: (0, i)),
            pl.BlockSpec((2 * PIECES, chunk), lambda i: (0, i)),
            pl.BlockSpec((2, 1, row_count, slab_width), lambda i: (1, 0, 0, 0)),
        ],
        out_specs=pl.BlockSpec((2, row_count, slab_width), lambda i: (0, 0, 0)),
        out_shape=jax.ShapeDtypeStruct((2, row_count, slab_width), jnp.float32),
        scratch_shapes=[pltpu.VMEM((row_count, width), jnp.float32)],
        compiler_params=pltpu.CompilerParams(vmem_limit_bytes=48 * 1024 * 1024),
        cost_estimate=pl.CostEstimate(
            flops=2 * row_count * width * drops, transcendentals=0, bytes_accessed=4 * row_count * width
        ),
    )(rows, cols, pieces, field)


def dft_tables(gx_count, slab_width):
    total_cells = gx_count * slab_width
    d_index = jnp.arange(gx_count, dtype=jnp.int32)
    j_index = jnp.arange(slab_width, dtype=jnp.int32)
    c64, s64 = phase(d_index[:, None] * d_index[None, :], gx_count)
    ct, st = phase(d_index[:, None] * j_index[None, :], total_cells)
    c128, s128 = phase(j_index[:, None] * j_index[None, :], slab_width)
    return d_index, j_index, c64, s64, ct, st, c128, s128


def fft_filter(spread, diffusivity, eigen_here, bulk_shift, tables):
    d_index, j_index, c64, s64, ct, st, c128, s128 = tables
    field_count, row_count, slab_width = spread.shape
    gx_count = c64.shape[0]
    rows_here = row_count // gx_count
    total_cells = gx_count * slab_width
    spread = spread.reshape(field_count, gx_count, rows_here, slab_width)

    a_real = jnp.einsum("kd,fdaj->fkaj", c64, spread, precision=EXACT)
    a_imag = -jnp.einsum("kd,fdaj->fkaj", s64, spread, precision=EXACT)
    ct4 = ct[None, :, None, :]
    st4 = st[None, :, None, :]
    b_real = a_real * ct4 + a_imag * st4
    b_imag = a_imag * ct4 - a_real * st4
    joined = jnp.concatenate([b_real, b_imag], axis=-1)
    forward_table = jnp.concatenate(
        [jnp.concatenate([c128, -s128], axis=1), jnp.concatenate([s128, c128], axis=1)], axis=0
    )
    spec = jnp.einsum("fkaj,jm->fkam", joined, forward_table, precision=EXACT)
    spec_real = spec[..., :slab_width]
    spec_imag = spec[..., slab_width:]

    mode_index = d_index[:, None] + gx_count * j_index[None, :]
    folded = jnp.minimum(mode_index, total_cells - mode_index).astype(jnp.float32)
    wavenumber = 2.0 * math.pi / total_cells * folded
    growth = diffusivity[:, None, None, None] * (
        eigen_here[None, None, :, None] + (wavenumber**2)[None, :, None, :]
    )
    damping = (1.0 - growth) / (1.0 + growth)
    signed = jnp.where(2 * mode_index >= total_cells, mode_index - total_cells, mode_index).astype(
        jnp.float32
    )
    travel = 2.0 * math.pi / total_cells * signed * bulk_shift[0]
    cos_travel = jnp.cos(travel)[None, :, None, :]
    sin_travel = jnp.sin(travel)[None, :, None, :]
    factor_real = damping * cos_travel
    factor_imag = -damping * sin_travel
    turned_real = spec_real * factor_real - spec_imag * factor_imag
    turned_imag = spec_real * factor_imag + spec_imag * factor_real

    joined = jnp.concatenate([turned_real, turned_imag], axis=-1)
    inverse_table = jnp.concatenate(
        [jnp.concatenate([c128, s128], axis=1), jnp.concatenate([-s128, c128], axis=1)], axis=0
    )
    back = jnp.einsum("fkam,mj->fkaj", joined, inverse_table, precision=EXACT)
    back_real = back[..., :slab_width]
    back_imag = back[..., slab_width:]
    e_real = back_real * ct4 - back_imag * st4
    e_imag = back_real * st4 + back_imag * ct4
    filtered = (
        jnp.einsum("dk,fkaj->fdaj", c64, e_real, precision=EXACT)
        - jnp.einsum("dk,fkaj->fdaj", s64, e_imag, precision=EXACT)
    ) / total_cells

    return filtered.reshape(field_count, row_count, slab_width)


def per_device(
    field,
    drop_cell,
    drop_plane,
    drop_rate,
    diffusivity,
    wall_eigen,
    basis_part,
    dual_part,
    bulk_shift,
):
    field_count, plane_count, row_count, slab_width = field.shape
    gx_count = lax.axis_size("gx")
    gz_count = lax.axis_size("gz")
    total_cells = slab_width * gx_count
    plane_cells = row_count * slab_width
    rows_here = row_count // gx_count

    plane_here = lax.axis_index("gz")
    packed = jnp.concatenate(
        [(drop_plane * plane_cells + drop_cell).astype(jnp.float32)[None, :], drop_rate], axis=0
    )
    shares = [packed] + [
        lax.ppermute(packed, "gz", [(i, (i + shift) % gz_count) for i in range(gz_count)])
        for shift in range(1, gz_count)
    ]
    packed = jnp.concatenate(shares, axis=1)
    keys = packed[0].astype(jnp.int32)
    cells = keys % plane_cells
    planes = keys // plane_cells
    rates = jnp.where((planes == plane_here)[None, :], packed[1:], 0.0)
    fed_side = drop_source(cells, rates, field)
    identity = jnp.eye(row_count, dtype=jnp.float32)
    dual_full = identity + dual_part
    calm = jnp.einsum("ay,fyx->fax", dual_full, field[:2, 0], precision=HI)
    calm = lax.all_to_all(calm, "gx", 1, 1, tiled=True)
    fed = jnp.einsum("ay,fyx->fax", dual_full, fed_side, precision=HI)
    fed = lax.all_to_all(fed, "gx", 1, 1, tiled=True)
    tables = dft_tables(gx_count, slab_width)
    position = lax.axis_index("gx")
    eigen_here = lax.dynamic_slice_in_dim(wall_eigen, position * rows_here, rows_here)
    calm = fft_filter(calm, diffusivity[:2], eigen_here, bulk_shift, tables)
    calm, fed = lax.optimization_barrier((calm, fed))
    fed = fft_filter(fed, diffusivity[2:], eigen_here, bulk_shift, tables)
    filtered = jnp.concatenate([calm, fed], axis=0)
    filtered = filtered.reshape(field_count, row_count, slab_width)
    gathered = lax.all_to_all(filtered, "gx", 1, 1, tiled=True)
    result = jnp.einsum("fax,ya->fyx", gathered, identity + basis_part, precision=HI)
    return result[:, None]


def solution(mesh):
    in_specs = (
        P(None, "gz", None, "gx"),
        P(("gx", "gz")),
        P(("gx", "gz")),
        P(None, ("gx", "gz")),
        P(),
        P(),
        P(),
        P(),
        P(),
    )
    out_specs = P(None, "gz", None, "gx")
    return jax.shard_map(
        per_device, mesh=mesh, in_specs=in_specs, out_specs=out_specs, check_vma=False
    )
```

```python
import math

import jax
import jax.numpy as jnp
from jax import lax
from jax.experimental import pallas as pl
from jax.experimental.pallas import tpu as pltpu
from jax.sharding import PartitionSpec as P

HI = lax.Precision.HIGH
EXACT = lax.Precision.HIGHEST


def phase(numer, length):
    angle = 2.0 * math.pi / length * (numer % length).astype(jnp.float32)
    return jnp.cos(angle), jnp.sin(angle)


PIECES = 2
CHUNK = 16384


def source_kernel(row_ref, col_ref, piece_ref, field_ref, out_ref, acc_ref):
    step = pl.program_id(0)
    row_count = acc_ref.shape[0]
    slab_width = out_ref.shape[2]
    chunk = row_ref.shape[1]
    rows = row_ref[...]
    cols = col_ref[...]
    row_hit = lax.broadcasted_iota(jnp.int32, (row_count, chunk), 0) == rows
    lhs = jnp.where(row_hit, 1.0, 0.0).astype(jnp.bfloat16)
    col_hit = lax.broadcasted_iota(jnp.int32, (slab_width, chunk), 0) == cols
    pieces = piece_ref[...]
    rhs = jnp.concatenate(
        [jnp.where(col_hit, pieces[p : p + 1, :], 0.0) for p in range(pieces.shape[0])], axis=0
    ).astype(jnp.bfloat16)
    part = lax.dot_general(
        lhs, rhs, (((1,), (1,)), ((), ())), preferred_element_type=jnp.float32
    )

    @pl.when(step == 0)
    def _():
        acc_ref[...] = part

    @pl.when(step > 0)
    def _():
        acc_ref[...] += part

    @pl.when(step == pl.num_programs(0) - 1)
    def _():
        for c in range(out_ref.shape[0]):
            total = field_ref[c, 0]
            for p in range(PIECES):
                start = (c * PIECES + p) * slab_width
                total = total + acc_ref[:, start : start + slab_width]
            out_ref[c] = total


def drop_source(cells, rates, field):
    drops = cells.shape[0]
    field_count, _, row_count, slab_width = field.shape
    pieces = []
    rest = rates
    for _ in range(PIECES):
        piece = lax.reduce_precision(rest, exponent_bits=8, mantissa_bits=7)
        pieces.append(piece)
        rest = rest - piece
    pieces = jnp.stack(pieces, axis=1).reshape(2 * PIECES, drops)
    rows = (cells // slab_width).reshape(1, drops)
    cols = (cells % slab_width).reshape(1, drops)
    width = 2 * PIECES * slab_width
    chunk = min(CHUNK, drops)
    return pl.pallas_call(
        source_kernel,
        grid=(drops // chunk,),
        in_specs=[
            pl.BlockSpec((1, chunk), lambda i: (0, i)),
            pl.BlockSpec((1, chunk), lambda i: (0, i)),
            pl.BlockSpec((2 * PIECES, chunk), lambda i: (0, i)),
            pl.BlockSpec((2, 1, row_count, slab_width), lambda i: (1, 0, 0, 0)),
        ],
        out_specs=pl.BlockSpec((2, row_count, slab_width), lambda i: (0, 0, 0)),
        out_shape=jax.ShapeDtypeStruct((2, row_count, slab_width), jnp.float32),
        scratch_shapes=[pltpu.VMEM((row_count, width), jnp.float32)],
        compiler_params=pltpu.CompilerParams(vmem_limit_bytes=48 * 1024 * 1024),
        cost_estimate=pl.CostEstimate(
            flops=2 * row_count * width * drops, transcendentals=0, bytes_accessed=4 * row_count * width
        ),
    )(rows, cols, pieces, field)


def dft_tables(gx_count, slab_width):
    total_cells = gx_count * slab_width
    d_index = jnp.arange(gx_count, dtype=jnp.int32)
    j_index = jnp.arange(slab_width, dtype=jnp.int32)
    c64, s64 = phase(d_index[:, None] * d_index[None, :], gx_count)
    ct, st = phase(d_index[:, None] * j_index[None, :], total_cells)
    c128, s128 = phase(j_index[:, None] * j_index[None, :], slab_width)
    return d_index, j_index, c64, s64, ct, st, c128, s128


def fft_filter(spread, diffusivity, eigen_here, bulk_shift, tables):
    d_index, j_index, c64, s64, ct, st, c128, s128 = tables
    gx_count, rows_here, field_count, slab_width = spread.shape
    total_cells = gx_count * slab_width
    stacked = jnp.concatenate([c64, -s64], axis=0)
    a_both = jnp.einsum("kd,dafj->kafj", stacked, spread, precision=EXACT)
    a_real = a_both[:gx_count]
    a_imag = a_both[gx_count:]
    ct4 = ct[:, None, None, :]
    st4 = st[:, None, None, :]
    b_real = a_real * ct4 + a_imag * st4
    b_imag = a_imag * ct4 - a_real * st4
    joined = jnp.concatenate([b_real, b_imag], axis=-1)
    forward_table = jnp.concatenate(
        [jnp.concatenate([c128, -s128], axis=1), jnp.concatenate([s128, c128], axis=1)], axis=0
    )
    spec = jnp.einsum("kafj,jm->kafm", joined, forward_table, precision=EXACT)
    spec_real = spec[..., :slab_width]
    spec_imag = spec[..., slab_width:]

    mode_index = d_index[:, None] + gx_count * j_index[None, :]
    folded = jnp.minimum(mode_index, total_cells - mode_index).astype(jnp.float32)
    wavenumber = 2.0 * math.pi / total_cells * folded
    growth = diffusivity[None, None, :, None] * (
        eigen_here[None, :, None, None] + (wavenumber**2)[:, None, None, :]
    )
    damping = (1.0 - growth) / (1.0 + growth)
    signed = jnp.where(2 * mode_index >= total_cells, mode_index - total_cells, mode_index).astype(
        jnp.float32
    )
    travel = 2.0 * math.pi / total_cells * signed * bulk_shift[0]
    cos_travel = jnp.cos(travel)[:, None, None, :]
    sin_travel = jnp.sin(travel)[:, None, None, :]
    factor_real = damping * cos_travel
    factor_imag = -damping * sin_travel
    turned_real = spec_real * factor_real - spec_imag * factor_imag
    turned_imag = spec_real * factor_imag + spec_imag * factor_real

    joined = jnp.concatenate([turned_real, turned_imag], axis=-1)
    inverse_table = jnp.concatenate(
        [jnp.concatenate([c128, s128], axis=1), jnp.concatenate([-s128, c128], axis=1)], axis=0
    )
    back = jnp.einsum("kafm,mj->kafj", joined, inverse_table, precision=EXACT)
    back_real = back[..., :slab_width]
    back_imag = back[..., slab_width:]
    e_real = back_real * ct4 - back_imag * st4
    e_imag = back_real * st4 + back_imag * ct4
    e_both = jnp.concatenate([e_real, e_imag], axis=0)
    unstack = jnp.concatenate([c64, -s64], axis=1)
    return jnp.einsum("dk,kafj->dafj", unstack, e_both, precision=EXACT) / total_cells


def per_device(
    field,
    drop_cell,
    drop_plane,
    drop_rate,
    diffusivity,
    wall_eigen,
    basis_part,
    dual_part,
    bulk_shift,
):
    field_count, plane_count, row_count, slab_width = field.shape
    gx_count = lax.axis_size("gx")
    gz_count = lax.axis_size("gz")
    total_cells = slab_width * gx_count
    plane_cells = row_count * slab_width
    rows_here = row_count // gx_count

    plane_here = lax.axis_index("gz")
    packed = jnp.concatenate(
        [(drop_plane * plane_cells + drop_cell).astype(jnp.float32)[None, :], drop_rate], axis=0
    )
    shares = [packed] + [
        lax.ppermute(packed, "gz", [(i, (i + shift) % gz_count) for i in range(gz_count)])
        for shift in range(1, gz_count)
    ]
    packed = jnp.concatenate(shares, axis=1)
    keys = packed[0].astype(jnp.int32)
    cells = keys % plane_cells
    planes = keys // plane_cells
    rates = jnp.where((planes == plane_here)[None, :], packed[1:], 0.0)
    fed_side = drop_source(cells, rates, field)
    identity = jnp.eye(row_count, dtype=jnp.float32)
    dual_full = identity + dual_part
    calm = jnp.einsum("ay,fyx->afx", dual_full, field[:2, 0], precision=HI)
    calm = lax.all_to_all(calm.reshape(row_count, -1), "gx", 0, 0, tiled=True)
    fed = jnp.einsum("ay,fyx->afx", dual_full, fed_side, precision=HI)
    fed = lax.all_to_all(fed.reshape(row_count, -1), "gx", 0, 0, tiled=True)
    tables = dft_tables(gx_count, slab_width)
    position = lax.axis_index("gx")
    eigen_here = lax.dynamic_slice_in_dim(wall_eigen, position * rows_here, rows_here)
    group_shape = (gx_count, rows_here, 2, slab_width)
    calm = fft_filter(calm.reshape(group_shape), diffusivity[:2], eigen_here, bulk_shift, tables)
    calm, fed = lax.optimization_barrier((calm, fed))
    fed = fft_filter(fed.reshape(group_shape), diffusivity[2:], eigen_here, bulk_shift, tables)
    filtered = jnp.concatenate([calm, fed], axis=2).reshape(row_count, field_count * slab_width)
    gathered = lax.all_to_all(filtered, "gx", 0, 0, tiled=True)
    gathered = gathered.reshape(row_count, field_count, slab_width)
    result = jnp.einsum("afx,ya->fyx", gathered, identity + basis_part, precision=HI)
    return result[:, None]


def solution(mesh):
    in_specs = (
        P(None, "gz", None, "gx"),
        P(("gx", "gz")),
        P(("gx", "gz")),
        P(None, ("gx", "gz")),
        P(),
        P(),
        P(),
        P(),
        P(),
    )
    out_specs = P(None, "gz", None, "gx")
    return jax.shard_map(
        per_device, mesh=mesh, in_specs=in_specs, out_specs=out_specs, check_vma=False
    )
```

```python
import math

import jax
import jax.numpy as jnp
from jax import lax
from jax.experimental import pallas as pl
from jax.experimental.pallas import tpu as pltpu
from jax.sharding import PartitionSpec as P

HI = lax.Precision.HIGH
EXACT = lax.Precision.HIGHEST


def phase(numer, length):
    angle = 2.0 * math.pi / length * (numer % length).astype(jnp.float32)
    return jnp.cos(angle), jnp.sin(angle)


PIECES = 2
CHUNK = 16384


def source_kernel(plane_ref, packed_ref, field_ref, out_ref, acc_ref):
    step = pl.program_id(0)
    row_count = acc_ref.shape[0]
    slab_width = out_ref.shape[2]
    chunk = packed_ref.shape[1]
    col_bits = slab_width.bit_length() - 1
    cell_bits = (row_count * slab_width).bit_length() - 1
    keys = packed_ref[0:1, :].astype(jnp.int32)
    mine = lax.shift_right_logical(keys, cell_bits) == plane_ref[0]
    rows = lax.shift_right_logical(keys & ((1 << cell_bits) - 1), col_bits)
    cols = keys & (slab_width - 1)
    row_hit = lax.broadcasted_iota(jnp.int32, (row_count, chunk), 0) == rows
    lhs = jnp.where(row_hit, 1.0, 0.0).astype(jnp.bfloat16)
    col_hit = lax.broadcasted_iota(jnp.int32, (slab_width, chunk), 0) == cols
    pieces = []
    for c in range(2):
        rest = jnp.where(mine, packed_ref[c + 1 : c + 2, :], 0.0)
        for _ in range(PIECES):
            piece = rest.astype(jnp.bfloat16).astype(jnp.float32)
            pieces.append(piece)
            rest = rest - piece
    rhs = jnp.concatenate([jnp.where(col_hit, p, 0.0) for p in pieces], axis=0).astype(
        jnp.bfloat16
    )
    part = lax.dot_general(
        lhs, rhs, (((1,), (1,)), ((), ())), preferred_element_type=jnp.float32
    )

    @pl.when(step == 0)
    def _():
        acc_ref[...] = part

    @pl.when(step > 0)
    def _():
        acc_ref[...] += part

    @pl.when(step == pl.num_programs(0) - 1)
    def _():
        for c in range(out_ref.shape[0]):
            total = field_ref[c, 0]
            for p in range(PIECES):
                start = (c * PIECES + p) * slab_width
                total = total + acc_ref[:, start : start + slab_width]
            out_ref[c] = total


def drop_source(packed, plane_here, field):
    drops = packed.shape[1]
    field_count, _, row_count, slab_width = field.shape
    width = 2 * PIECES * slab_width
    chunk = min(CHUNK, drops)
    return pl.pallas_call(
        source_kernel,
        grid=(drops // chunk,),
        in_specs=[
            pl.BlockSpec(memory_space=pltpu.SMEM),
            pl.BlockSpec((packed.shape[0], chunk), lambda i: (0, i)),
            pl.BlockSpec((2, 1, row_count, slab_width), lambda i: (1, 0, 0, 0)),
        ],
        out_specs=pl.BlockSpec((2, row_count, slab_width), lambda i: (0, 0, 0)),
        out_shape=jax.ShapeDtypeStruct((2, row_count, slab_width), jnp.float32),
        scratch_shapes=[pltpu.VMEM((row_count, width), jnp.float32)],
        compiler_params=pltpu.CompilerParams(vmem_limit_bytes=48 * 1024 * 1024),
        cost_estimate=pl.CostEstimate(
            flops=2 * row_count * width * drops, transcendentals=0, bytes_accessed=4 * row_count * width
        ),
    )(plane_here.reshape(1), packed, field)


def dft_tables(gx_count, slab_width):
    total_cells = gx_count * slab_width
    d_index = jnp.arange(gx_count, dtype=jnp.int32)
    j_index = jnp.arange(slab_width, dtype=jnp.int32)
    c64, s64 = phase(d_index[:, None] * d_index[None, :], gx_count)
    ct, st = phase(d_index[:, None] * j_index[None, :], total_cells)
    c128, s128 = phase(j_index[:, None] * j_index[None, :], slab_width)
    return d_index, j_index, c64, s64, ct, st, c128, s128


def fft_filter(spread, diffusivity, eigen_here, bulk_shift, tables):
    d_index, j_index, c64, s64, ct, st, c128, s128 = tables
    field_count, row_count, slab_width = spread.shape
    gx_count = c64.shape[0]
    rows_here = row_count // gx_count
    total_cells = gx_count * slab_width
    spread = spread.reshape(field_count, gx_count, rows_here, slab_width)

    a_real = jnp.einsum("kd,fdaj->fkaj", c64, spread, precision=EXACT)
    a_imag = -jnp.einsum("kd,fdaj->fkaj", s64, spread, precision=EXACT)
    ct4 = ct[None, :, None, :]
    st4 = st[None, :, None, :]
    b_real = a_real * ct4 + a_imag * st4
    b_imag = a_imag * ct4 - a_real * st4
    joined = jnp.concatenate([b_real, b_imag], axis=-1)
    forward_table = jnp.concatenate(
        [jnp.concatenate([c128, -s128], axis=1), jnp.concatenate([s128, c128], axis=1)], axis=0
    )
    spec = jnp.einsum("fkaj,jm->fkam", joined, forward_table, precision=EXACT)
    spec_real = spec[..., :slab_width]
    spec_imag = spec[..., slab_width:]

    mode_index = d_index[:, None] + gx_count * j_index[None, :]
    folded = jnp.minimum(mode_index, total_cells - mode_index).astype(jnp.float32)
    wavenumber = 2.0 * math.pi / total_cells * folded
    growth = diffusivity[:, None, None, None] * (
        eigen_here[None, None, :, None] + (wavenumber**2)[None, :, None, :]
    )
    damping = (1.0 - growth) / (1.0 + growth)
    signed = jnp.where(2 * mode_index >= total_cells, mode_index - total_cells, mode_index).astype(
        jnp.float32
    )
    travel = 2.0 * math.pi / total_cells * signed * bulk_shift[0]
    cos_travel = jnp.cos(travel)[None, :, None, :]
    sin_travel = jnp.sin(travel)[None, :, None, :]
    factor_real = damping * cos_travel
    factor_imag = -damping * sin_travel
    turned_real = spec_real * factor_real - spec_imag * factor_imag
    turned_imag = spec_real * factor_imag + spec_imag * factor_real

    joined = jnp.concatenate([turned_real, turned_imag], axis=-1)
    inverse_table = jnp.concatenate(
        [jnp.concatenate([c128, s128], axis=1), jnp.concatenate([-s128, c128], axis=1)], axis=0
    )
    back = jnp.einsum("fkam,mj->fkaj", joined, inverse_table, precision=EXACT)
    back_real = back[..., :slab_width]
    back_imag = back[..., slab_width:]
    e_real = back_real * ct4 - back_imag * st4
    e_imag = back_real * st4 + back_imag * ct4
    filtered = (
        jnp.einsum("dk,fkaj->fdaj", c64, e_real, precision=EXACT)
        - jnp.einsum("dk,fkaj->fdaj", s64, e_imag, precision=EXACT)
    ) / total_cells

    return filtered.reshape(field_count, row_count, slab_width)


def per_device(
    field,
    drop_cell,
    drop_plane,
    drop_rate,
    diffusivity,
    wall_eigen,
    basis_part,
    dual_part,
    bulk_shift,
):
    field_count, plane_count, row_count, slab_width = field.shape
    gx_count = lax.axis_size("gx")
    gz_count = lax.axis_size("gz")
    total_cells = slab_width * gx_count
    plane_cells = row_count * slab_width
    rows_here = row_count // gx_count

    plane_here = lax.axis_index("gz")
    packed = jnp.concatenate(
        [(drop_plane * plane_cells + drop_cell).astype(jnp.float32)[None, :], drop_rate], axis=0
    )
    shares = [packed] + [
        lax.ppermute(packed, "gz", [(i, (i + shift) % gz_count) for i in range(gz_count)])
        for shift in range(1, gz_count)
    ]
    packed = jnp.concatenate(shares, axis=1)
    fed_side = drop_source(packed, plane_here.astype(jnp.int32), field)
    identity = jnp.eye(row_count, dtype=jnp.float32)
    dual_full = identity + dual_part
    calm = jnp.einsum("ay,fyx->fax", dual_full, field[:2, 0], precision=HI)
    calm = lax.all_to_all(calm, "gx", 1, 1, tiled=True)
    fed = jnp.einsum("ay,fyx->fax", dual_full, fed_side, precision=HI)
    fed = lax.all_to_all(fed, "gx", 1, 1, tiled=True)
    tables = dft_tables(gx_count, slab_width)
    position = lax.axis_index("gx")
    eigen_here = lax.dynamic_slice_in_dim(wall_eigen, position * rows_here, rows_here)
    calm = fft_filter(calm, diffusivity[:2], eigen_here, bulk_shift, tables)
    calm, fed = lax.optimization_barrier((calm, fed))
    fed = fft_filter(fed, diffusivity[2:], eigen_here, bulk_shift, tables)
    filtered = jnp.concatenate([calm, fed], axis=0)
    filtered = filtered.reshape(field_count, row_count, slab_width)
    gathered = lax.all_to_all(filtered, "gx", 1, 1, tiled=True)
    result = jnp.einsum("fax,ya->fyx", gathered, identity + basis_part, precision=HI)
    return result[:, None]


def solution(mesh):
    in_specs = (
        P(None, "gz", None, "gx"),
        P(("gx", "gz")),
        P(("gx", "gz")),
        P(None, ("gx", "gz")),
        P(),
        P(),
        P(),
        P(),
        P(),
    )
    out_specs = P(None, "gz", None, "gx")
    return jax.shard_map(
        per_device, mesh=mesh, in_specs=in_specs, out_specs=out_specs, check_vma=False
    )
```

```python
import math

import jax
import jax.numpy as jnp
from jax import lax
from jax.experimental import pallas as pl
from jax.experimental.pallas import tpu as pltpu
from jax.sharding import PartitionSpec as P

HI = lax.Precision.HIGH
EXACT = lax.Precision.HIGHEST


def phase(numer, length):
    angle = 2.0 * math.pi / length * (numer % length).astype(jnp.float32)
    return jnp.cos(angle), jnp.sin(angle)


PIECES = 2
CHUNK = 16384


def source_kernel(plane_ref, packed_ref, field_ref, out_ref, acc_ref):
    step = pl.program_id(0)
    row_count = acc_ref.shape[0]
    slab_width = out_ref.shape[2]
    chunk = packed_ref.shape[1]
    col_bits = slab_width.bit_length() - 1
    cell_bits = (row_count * slab_width).bit_length() - 1
    keys = packed_ref[0:1, :].astype(jnp.int32)
    mine = lax.shift_right_logical(keys, cell_bits) == plane_ref[0]
    rows = lax.shift_right_logical(keys & ((1 << cell_bits) - 1), col_bits)
    cols = keys & (slab_width - 1)
    row_hit = lax.broadcasted_iota(jnp.int32, (row_count, chunk), 0) == rows
    lhs = jnp.where(row_hit, 1.0, 0.0).astype(jnp.bfloat16)
    col_hit = lax.broadcasted_iota(jnp.int32, (slab_width, chunk), 0) == cols
    pieces = []
    for c in range(2):
        rest = jnp.where(mine, packed_ref[c + 1 : c + 2, :], 0.0)
        for _ in range(PIECES):
            piece = rest.astype(jnp.bfloat16).astype(jnp.float32)
            pieces.append(piece)
            rest = rest - piece
    rhs = jnp.concatenate([jnp.where(col_hit, p, 0.0) for p in pieces], axis=0).astype(
        jnp.bfloat16
    )
    part = lax.dot_general(
        lhs, rhs, (((1,), (1,)), ((), ())), preferred_element_type=jnp.float32
    )

    @pl.when(step == 0)
    def _():
        acc_ref[...] = part

    @pl.when(step > 0)
    def _():
        acc_ref[...] += part

    @pl.when(step == pl.num_programs(0) - 1)
    def _():
        for c in range(out_ref.shape[0]):
            total = field_ref[c, 0]
            for p in range(PIECES):
                start = (c * PIECES + p) * slab_width
                total = total + acc_ref[:, start : start + slab_width]
            out_ref[c] = total


def drop_source(packed, plane_here, field):
    drops = packed.shape[1]
    field_count, _, row_count, slab_width = field.shape
    width = 2 * PIECES * slab_width
    chunk = min(CHUNK, drops)
    return pl.pallas_call(
        source_kernel,
        grid=(drops // chunk,),
        in_specs=[
            pl.BlockSpec(memory_space=pltpu.SMEM),
            pl.BlockSpec((packed.shape[0], chunk), lambda i: (0, i)),
            pl.BlockSpec((2, 1, row_count, slab_width), lambda i: (1, 0, 0, 0)),
        ],
        out_specs=pl.BlockSpec((2, row_count, slab_width), lambda i: (0, 0, 0)),
        out_shape=jax.ShapeDtypeStruct((2, row_count, slab_width), jnp.float32),
        scratch_shapes=[pltpu.VMEM((row_count, width), jnp.float32)],
        compiler_params=pltpu.CompilerParams(vmem_limit_bytes=48 * 1024 * 1024),
        cost_estimate=pl.CostEstimate(
            flops=2 * row_count * width * drops, transcendentals=0, bytes_accessed=4 * row_count * width
        ),
    )(plane_here.reshape(1), packed, field)


def dft_tables(gx_count, slab_width):
    total_cells = gx_count * slab_width
    d_index = jnp.arange(gx_count, dtype=jnp.int32)
    j_index = jnp.arange(slab_width, dtype=jnp.int32)
    c64, s64 = phase(d_index[:, None] * d_index[None, :], gx_count)
    ct, st = phase(d_index[:, None] * j_index[None, :], total_cells)
    c128, s128 = phase(j_index[:, None] * j_index[None, :], slab_width)
    return d_index, j_index, c64, s64, ct, st, c128, s128


def fft_filter(spread, diffusivity, eigen_here, bulk_shift, tables):
    d_index, j_index, c64, s64, ct, st, c128, s128 = tables
    field_count, row_count, slab_width = spread.shape
    gx_count = c64.shape[0]
    rows_here = row_count // gx_count
    total_cells = gx_count * slab_width
    spread = spread.reshape(field_count, gx_count, rows_here, slab_width)

    a_real = jnp.einsum("kd,fdaj->fkaj", c64, spread, precision=EXACT)
    a_imag = -jnp.einsum("kd,fdaj->fkaj", s64, spread, precision=EXACT)
    ct4 = ct[None, :, None, :]
    st4 = st[None, :, None, :]
    b_real = a_real * ct4 + a_imag * st4
    b_imag = a_imag * ct4 - a_real * st4
    joined = jnp.concatenate([b_real, b_imag], axis=-1)
    forward_table = jnp.concatenate(
        [jnp.concatenate([c128, -s128], axis=1), jnp.concatenate([s128, c128], axis=1)], axis=0
    )
    spec = jnp.einsum("fkaj,jm->fkam", joined, forward_table, precision=EXACT)
    spec_real = spec[..., :slab_width]
    spec_imag = spec[..., slab_width:]

    mode_index = d_index[:, None] + gx_count * j_index[None, :]
    folded = jnp.minimum(mode_index, total_cells - mode_index).astype(jnp.float32)
    wavenumber = 2.0 * math.pi / total_cells * folded
    growth = diffusivity[:, None, None, None] * (
        eigen_here[None, None, :, None] + (wavenumber**2)[None, :, None, :]
    )
    damping = (1.0 - growth) / (1.0 + growth)
    signed = jnp.where(2 * mode_index >= total_cells, mode_index - total_cells, mode_index).astype(
        jnp.float32
    )
    travel = 2.0 * math.pi / total_cells * signed * bulk_shift[0]
    cos_travel = jnp.cos(travel)[None, :, None, :]
    sin_travel = jnp.sin(travel)[None, :, None, :]
    factor_real = damping * cos_travel
    factor_imag = -damping * sin_travel
    turned_real = spec_real * factor_real - spec_imag * factor_imag
    turned_imag = spec_real * factor_imag + spec_imag * factor_real

    joined = jnp.concatenate([turned_real, turned_imag], axis=-1)
    inverse_table = jnp.concatenate(
        [jnp.concatenate([c128, s128], axis=1), jnp.concatenate([-s128, c128], axis=1)], axis=0
    )
    back = jnp.einsum("fkam,mj->fkaj", joined, inverse_table, precision=EXACT)
    back_real = back[..., :slab_width]
    back_imag = back[..., slab_width:]
    e_real = back_real * ct4 - back_imag * st4
    e_imag = back_real * st4 + back_imag * ct4
    filtered = (
        jnp.einsum("dk,fkaj->fdaj", c64, e_real, precision=EXACT)
        - jnp.einsum("dk,fkaj->fdaj", s64, e_imag, precision=EXACT)
    ) / total_cells

    return filtered.reshape(field_count, row_count, slab_width)


def per_device(
    field,
    drop_cell,
    drop_plane,
    drop_rate,
    diffusivity,
    wall_eigen,
    basis_part,
    dual_part,
    bulk_shift,
):
    field_count, plane_count, row_count, slab_width = field.shape
    gx_count = lax.axis_size("gx")
    gz_count = lax.axis_size("gz")
    total_cells = slab_width * gx_count
    plane_cells = row_count * slab_width
    rows_here = row_count // gx_count

    plane_here = lax.axis_index("gz")
    packed = jnp.concatenate(
        [(drop_plane * plane_cells + drop_cell).astype(jnp.float32)[None, :], drop_rate], axis=0
    )
    slots = jnp.arange(gz_count, dtype=jnp.int32)[:, None, None] == plane_here
    packed = lax.psum(jnp.where(slots, packed[None], 0.0), "gz")
    packed = jnp.transpose(packed, (1, 0, 2)).reshape(packed.shape[1], -1)
    fed_side = drop_source(packed, plane_here.astype(jnp.int32), field)
    identity = jnp.eye(row_count, dtype=jnp.float32)
    dual_full = identity + dual_part
    calm = jnp.einsum("ay,fyx->fax", dual_full, field[:2, 0], precision=HI)
    calm = lax.all_to_all(calm, "gx", 1, 1, tiled=True)
    fed = jnp.einsum("ay,fyx->fax", dual_full, fed_side, precision=HI)
    fed = lax.all_to_all(fed, "gx", 1, 1, tiled=True)
    tables = dft_tables(gx_count, slab_width)
    position = lax.axis_index("gx")
    eigen_here = lax.dynamic_slice_in_dim(wall_eigen, position * rows_here, rows_here)
    calm = fft_filter(calm, diffusivity[:2], eigen_here, bulk_shift, tables)
    calm, fed = lax.optimization_barrier((calm, fed))
    fed = fft_filter(fed, diffusivity[2:], eigen_here, bulk_shift, tables)
    filtered = jnp.concatenate([calm, fed], axis=0)
    filtered = filtered.reshape(field_count, row_count, slab_width)
    gathered = lax.all_to_all(filtered, "gx", 1, 1, tiled=True)
    result = jnp.einsum("fax,ya->fyx", gathered, identity + basis_part, precision=HI)
    return result[:, None]


def solution(mesh):
    in_specs = (
        P(None, "gz", None, "gx"),
        P(("gx", "gz")),
        P(("gx", "gz")),
        P(None, ("gx", "gz")),
        P(),
        P(),
        P(),
        P(),
        P(),
    )
    out_specs = P(None, "gz", None, "gx")
    return jax.shard_map(
        per_device, mesh=mesh, in_specs=in_specs, out_specs=out_specs, check_vma=False
    )
```

```python
import math

import jax
import jax.numpy as jnp
from jax import lax
from jax.experimental import pallas as pl
from jax.experimental.pallas import tpu as pltpu
from jax.sharding import PartitionSpec as P

HI = lax.Precision.HIGH
EXACT = lax.Precision.HIGHEST


def phase(numer, length):
    angle = 2.0 * math.pi / length * (numer % length).astype(jnp.float32)
    return jnp.cos(angle), jnp.sin(angle)


PIECES = 2
CHUNK = 16384


def source_kernel(plane_ref, packed_ref, field_ref, out_ref, acc_ref):
    step = pl.program_id(0)
    row_count = acc_ref.shape[0]
    slab_width = out_ref.shape[2]
    chunk = packed_ref.shape[1]
    col_bits = slab_width.bit_length() - 1
    cell_bits = (row_count * slab_width).bit_length() - 1
    keys = packed_ref[0:1, :].astype(jnp.int32)
    mine = lax.shift_right_logical(keys, cell_bits) == plane_ref[0]
    rows = lax.shift_right_logical(keys & ((1 << cell_bits) - 1), col_bits)
    cols = keys & (slab_width - 1)
    row_hit = lax.broadcasted_iota(jnp.int32, (row_count, chunk), 0) == rows
    lhs = jnp.where(row_hit, 1.0, 0.0).astype(jnp.bfloat16)
    col_hit = lax.broadcasted_iota(jnp.int32, (slab_width, chunk), 0) == cols
    pieces = []
    for c in range(2):
        rest = jnp.where(mine, packed_ref[c + 1 : c + 2, :], 0.0)
        for _ in range(PIECES):
            piece = rest.astype(jnp.bfloat16).astype(jnp.float32)
            pieces.append(piece)
            rest = rest - piece
    rhs = jnp.concatenate([jnp.where(col_hit, p, 0.0) for p in pieces], axis=0).astype(
        jnp.bfloat16
    )
    part = lax.dot_general(
        lhs, rhs, (((1,), (1,)), ((), ())), preferred_element_type=jnp.float32
    )

    @pl.when(step == 0)
    def _():
        acc_ref[...] = part

    @pl.when(step > 0)
    def _():
        acc_ref[...] += part

    @pl.when(step == pl.num_programs(0) - 1)
    def _():
        for c in range(out_ref.shape[0]):
            total = field_ref[c, 0]
            for p in range(PIECES):
                start = (c * PIECES + p) * slab_width
                total = total + acc_ref[:, start : start + slab_width]
            out_ref[c] = total


def drop_source(packed, plane_here, field):
    drops = packed.shape[1]
    field_count, _, row_count, slab_width = field.shape
    width = 2 * PIECES * slab_width
    chunk = min(CHUNK, drops)
    return pl.pallas_call(
        source_kernel,
        grid=(drops // chunk,),
        in_specs=[
            pl.BlockSpec(memory_space=pltpu.SMEM),
            pl.BlockSpec((packed.shape[0], chunk), lambda i: (0, i)),
            pl.BlockSpec((2, 1, row_count, slab_width), lambda i: (1, 0, 0, 0)),
        ],
        out_specs=pl.BlockSpec((2, row_count, slab_width), lambda i: (0, 0, 0)),
        out_shape=jax.ShapeDtypeStruct((2, row_count, slab_width), jnp.float32),
        scratch_shapes=[pltpu.VMEM((row_count, width), jnp.float32)],
        compiler_params=pltpu.CompilerParams(vmem_limit_bytes=48 * 1024 * 1024),
        cost_estimate=pl.CostEstimate(
            flops=2 * row_count * width * drops, transcendentals=0, bytes_accessed=4 * row_count * width
        ),
    )(plane_here.reshape(1), packed, field)


def dft_tables(gx_count, slab_width):
    total_cells = gx_count * slab_width
    d_index = jnp.arange(gx_count, dtype=jnp.int32)
    j_index = jnp.arange(slab_width, dtype=jnp.int32)
    c64, s64 = phase(d_index[:, None] * d_index[None, :], gx_count)
    ct, st = phase(d_index[:, None] * j_index[None, :], total_cells)
    c128, s128 = phase(j_index[:, None] * j_index[None, :], slab_width)
    return d_index, j_index, c64, s64, ct, st, c128, s128


def fft_filter(spread, diffusivity, eigen_here, bulk_shift, tables):
    d_index, j_index, c64, s64, ct, st, c128, s128 = tables
    field_count, row_count, slab_width = spread.shape
    gx_count = c64.shape[0]
    rows_here = row_count // gx_count
    total_cells = gx_count * slab_width
    spread = spread.reshape(field_count, gx_count, rows_here, slab_width)

    a_real = jnp.einsum("kd,fdaj->fkaj", c64, spread, precision=EXACT)
    a_imag = -jnp.einsum("kd,fdaj->fkaj", s64, spread, precision=EXACT)
    ct4 = ct[None, :, None, :]
    st4 = st[None, :, None, :]
    b_real = a_real * ct4 + a_imag * st4
    b_imag = a_imag * ct4 - a_real * st4
    joined = jnp.concatenate([b_real, b_imag], axis=-1)
    forward_table = jnp.concatenate(
        [jnp.concatenate([c128, -s128], axis=1), jnp.concatenate([s128, c128], axis=1)], axis=0
    )
    spec = jnp.einsum("fkaj,jm->fkam", joined, forward_table, precision=EXACT)
    spec_real = spec[..., :slab_width]
    spec_imag = spec[..., slab_width:]

    mode_index = d_index[:, None] + gx_count * j_index[None, :]
    folded = jnp.minimum(mode_index, total_cells - mode_index).astype(jnp.float32)
    wavenumber = 2.0 * math.pi / total_cells * folded
    growth = diffusivity[:, None, None, None] * (
        eigen_here[None, None, :, None] + (wavenumber**2)[None, :, None, :]
    )
    damping = (1.0 - growth) / (1.0 + growth)
    signed = jnp.where(2 * mode_index >= total_cells, mode_index - total_cells, mode_index).astype(
        jnp.float32
    )
    travel = 2.0 * math.pi / total_cells * signed * bulk_shift[0]
    cos_travel = jnp.cos(travel)[None, :, None, :]
    sin_travel = jnp.sin(travel)[None, :, None, :]
    factor_real = damping * cos_travel
    factor_imag = -damping * sin_travel
    turned_real = spec_real * factor_real - spec_imag * factor_imag
    turned_imag = spec_real * factor_imag + spec_imag * factor_real

    joined = jnp.concatenate([turned_real, turned_imag], axis=-1)
    inverse_table = jnp.concatenate(
        [jnp.concatenate([c128, s128], axis=1), jnp.concatenate([-s128, c128], axis=1)], axis=0
    )
    back = jnp.einsum("fkam,mj->fkaj", joined, inverse_table, precision=EXACT)
    back_real = back[..., :slab_width]
    back_imag = back[..., slab_width:]
    e_real = back_real * ct4 - back_imag * st4
    e_imag = back_real * st4 + back_imag * ct4
    filtered = (
        jnp.einsum("dk,fkaj->fdaj", c64, e_real, precision=EXACT)
        - jnp.einsum("dk,fkaj->fdaj", s64, e_imag, precision=EXACT)
    ) / total_cells

    return filtered.reshape(field_count, row_count, slab_width)


def per_device(
    field,
    drop_cell,
    drop_plane,
    drop_rate,
    diffusivity,
    wall_eigen,
    basis_part,
    dual_part,
    bulk_shift,
):
    field_count, plane_count, row_count, slab_width = field.shape
    gx_count = lax.axis_size("gx")
    gz_count = lax.axis_size("gz")
    total_cells = slab_width * gx_count
    plane_cells = row_count * slab_width
    rows_here = row_count // gx_count

    plane_here = lax.axis_index("gz")
    packed = jnp.concatenate(
        [(drop_plane * plane_cells + drop_cell).astype(jnp.float32)[None, :], drop_rate], axis=0
    )
    span = 1
    while span < gz_count:
        partner = lax.ppermute(packed, "gz", [(i, i ^ span) for i in range(gz_count)])
        packed = jnp.concatenate([packed, partner], axis=1)
        span *= 2
    fed_side = drop_source(packed, plane_here.astype(jnp.int32), field)
    identity = jnp.eye(row_count, dtype=jnp.float32)
    dual_full = identity + dual_part
    calm = jnp.einsum("ay,fyx->fax", dual_full, field[:2, 0], precision=HI)
    calm = lax.all_to_all(calm, "gx", 1, 1, tiled=True)
    fed = jnp.einsum("ay,fyx->fax", dual_full, fed_side, precision=HI)
    fed = lax.all_to_all(fed, "gx", 1, 1, tiled=True)
    tables = dft_tables(gx_count, slab_width)
    position = lax.axis_index("gx")
    eigen_here = lax.dynamic_slice_in_dim(wall_eigen, position * rows_here, rows_here)
    calm = fft_filter(calm, diffusivity[:2], eigen_here, bulk_shift, tables)
    calm, fed = lax.optimization_barrier((calm, fed))
    fed = fft_filter(fed, diffusivity[2:], eigen_here, bulk_shift, tables)
    filtered = jnp.concatenate([calm, fed], axis=0)
    filtered = filtered.reshape(field_count, row_count, slab_width)
    gathered = lax.all_to_all(filtered, "gx", 1, 1, tiled=True)
    result = jnp.einsum("fax,ya->fyx", gathered, identity + basis_part, precision=HI)
    return result[:, None]


def solution(mesh):
    in_specs = (
        P(None, "gz", None, "gx"),
        P(("gx", "gz")),
        P(("gx", "gz")),
        P(None, ("gx", "gz")),
        P(),
        P(),
        P(),
        P(),
        P(),
    )
    out_specs = P(None, "gz", None, "gx")
    return jax.shard_map(
        per_device, mesh=mesh, in_specs=in_specs, out_specs=out_specs, check_vma=False
    )
```

```python
import math

import jax
import jax.numpy as jnp
from jax import lax
from jax.experimental import pallas as pl
from jax.experimental.pallas import tpu as pltpu
from jax.sharding import PartitionSpec as P

HI = lax.Precision.HIGH
EXACT = lax.Precision.HIGHEST


def phase(numer, length):
    angle = 2.0 * math.pi / length * (numer % length).astype(jnp.float32)
    return jnp.cos(angle), jnp.sin(angle)


PIECES = 2
CHUNK = 16384


def source_kernel(plane_ref, packed_ref, field_ref, out_ref, acc_ref):
    step = pl.program_id(0)
    row_count = acc_ref.shape[0]
    slab_width = out_ref.shape[2]
    chunk = packed_ref.shape[1]
    col_bits = slab_width.bit_length() - 1
    cell_bits = (row_count * slab_width).bit_length() - 1
    keys = packed_ref[0:1, :].astype(jnp.int32)
    mine = lax.shift_right_logical(keys, cell_bits) == plane_ref[0]
    rows = lax.shift_right_logical(keys & ((1 << cell_bits) - 1), col_bits)
    cols = keys & (slab_width - 1)
    row_hit = lax.broadcasted_iota(jnp.int32, (row_count, chunk), 0) == rows
    lhs = jnp.where(row_hit, 1.0, 0.0).astype(jnp.bfloat16)
    col_hit = lax.broadcasted_iota(jnp.int32, (slab_width, chunk), 0) == cols
    pieces = []
    for c in range(2):
        rest = jnp.where(mine, packed_ref[c + 1 : c + 2, :], 0.0)
        for _ in range(PIECES):
            piece = rest.astype(jnp.bfloat16).astype(jnp.float32)
            pieces.append(piece)
            rest = rest - piece
    rhs = jnp.concatenate([jnp.where(col_hit, p, 0.0) for p in pieces], axis=0).astype(
        jnp.bfloat16
    )
    part = lax.dot_general(
        lhs, rhs, (((1,), (1,)), ((), ())), preferred_element_type=jnp.float32
    )

    @pl.when(step == 0)
    def _():
        acc_ref[...] = part

    @pl.when(step > 0)
    def _():
        acc_ref[...] += part

    @pl.when(step == pl.num_programs(0) - 1)
    def _():
        for c in range(out_ref.shape[0]):
            total = field_ref[c, 0]
            for p in range(PIECES):
                start = (c * PIECES + p) * slab_width
                total = total + acc_ref[:, start : start + slab_width]
            out_ref[c] = total


def drop_source(packed, plane_here, field):
    drops = packed.shape[1]
    field_count, _, row_count, slab_width = field.shape
    width = 2 * PIECES * slab_width
    chunk = min(CHUNK, drops)
    return pl.pallas_call(
        source_kernel,
        grid=(drops // chunk,),
        in_specs=[
            pl.BlockSpec(memory_space=pltpu.SMEM),
            pl.BlockSpec((packed.shape[0], chunk), lambda i: (0, i)),
            pl.BlockSpec((2, 1, row_count, slab_width), lambda i: (1, 0, 0, 0)),
        ],
        out_specs=pl.BlockSpec((2, row_count, slab_width), lambda i: (0, 0, 0)),
        out_shape=jax.ShapeDtypeStruct((2, row_count, slab_width), jnp.float32),
        scratch_shapes=[pltpu.VMEM((row_count, width), jnp.float32)],
        compiler_params=pltpu.CompilerParams(vmem_limit_bytes=48 * 1024 * 1024),
        cost_estimate=pl.CostEstimate(
            flops=2 * row_count * width * drops, transcendentals=0, bytes_accessed=4 * row_count * width
        ),
    )(plane_here.reshape(1), packed, field)


def dft_tables(gx_count, slab_width):
    total_cells = gx_count * slab_width
    d_index = jnp.arange(gx_count, dtype=jnp.int32)
    j_index = jnp.arange(slab_width, dtype=jnp.int32)
    c64, s64 = phase(d_index[:, None] * d_index[None, :], gx_count)
    ct, st = phase(d_index[:, None] * j_index[None, :], total_cells)
    c128, s128 = phase(j_index[:, None] * j_index[None, :], slab_width)
    return d_index, j_index, c64, s64, ct, st, c128, s128


def fft_filter(spread, diffusivity, eigen_here, bulk_shift, tables, precision):
    d_index, j_index, c64, s64, ct, st, c128, s128 = tables
    field_count, row_count, slab_width = spread.shape
    gx_count = c64.shape[0]
    rows_here = row_count // gx_count
    total_cells = gx_count * slab_width
    spread = spread.reshape(field_count, gx_count, rows_here, slab_width)

    a_real = jnp.einsum("kd,fdaj->fkaj", c64, spread, precision=precision)
    a_imag = -jnp.einsum("kd,fdaj->fkaj", s64, spread, precision=precision)
    ct4 = ct[None, :, None, :]
    st4 = st[None, :, None, :]
    b_real = a_real * ct4 + a_imag * st4
    b_imag = a_imag * ct4 - a_real * st4
    joined = jnp.concatenate([b_real, b_imag], axis=-1)
    forward_table = jnp.concatenate(
        [jnp.concatenate([c128, -s128], axis=1), jnp.concatenate([s128, c128], axis=1)], axis=0
    )
    spec = jnp.einsum("fkaj,jm->fkam", joined, forward_table, precision=precision)
    spec_real = spec[..., :slab_width]
    spec_imag = spec[..., slab_width:]

    mode_index = d_index[:, None] + gx_count * j_index[None, :]
    folded = jnp.minimum(mode_index, total_cells - mode_index).astype(jnp.float32)
    wavenumber = 2.0 * math.pi / total_cells * folded
    growth = diffusivity[:, None, None, None] * (
        eigen_here[None, None, :, None] + (wavenumber**2)[None, :, None, :]
    )
    damping = (1.0 - growth) / (1.0 + growth)
    signed = jnp.where(2 * mode_index >= total_cells, mode_index - total_cells, mode_index).astype(
        jnp.float32
    )
    travel = 2.0 * math.pi / total_cells * signed * bulk_shift[0]
    cos_travel = jnp.cos(travel)[None, :, None, :]
    sin_travel = jnp.sin(travel)[None, :, None, :]
    factor_real = damping * cos_travel
    factor_imag = -damping * sin_travel
    turned_real = spec_real * factor_real - spec_imag * factor_imag
    turned_imag = spec_real * factor_imag + spec_imag * factor_real

    joined = jnp.concatenate([turned_real, turned_imag], axis=-1)
    inverse_table = jnp.concatenate(
        [jnp.concatenate([c128, s128], axis=1), jnp.concatenate([-s128, c128], axis=1)], axis=0
    )
    back = jnp.einsum("fkam,mj->fkaj", joined, inverse_table, precision=precision)
    back_real = back[..., :slab_width]
    back_imag = back[..., slab_width:]
    e_real = back_real * ct4 - back_imag * st4
    e_imag = back_real * st4 + back_imag * ct4
    filtered = (
        jnp.einsum("dk,fkaj->fdaj", c64, e_real, precision=precision)
        - jnp.einsum("dk,fkaj->fdaj", s64, e_imag, precision=precision)
    ) / total_cells

    return filtered.reshape(field_count, row_count, slab_width)


def per_device(
    field,
    drop_cell,
    drop_plane,
    drop_rate,
    diffusivity,
    wall_eigen,
    basis_part,
    dual_part,
    bulk_shift,
):
    field_count, plane_count, row_count, slab_width = field.shape
    gx_count = lax.axis_size("gx")
    gz_count = lax.axis_size("gz")
    total_cells = slab_width * gx_count
    plane_cells = row_count * slab_width
    rows_here = row_count // gx_count

    plane_here = lax.axis_index("gz")
    packed = jnp.concatenate(
        [(drop_plane * plane_cells + drop_cell).astype(jnp.float32)[None, :], drop_rate], axis=0
    )
    shares = [packed] + [
        lax.ppermute(packed, "gz", [(i, (i + shift) % gz_count) for i in range(gz_count)])
        for shift in range(1, gz_count)
    ]
    packed = jnp.concatenate(shares, axis=1)
    fed_side = drop_source(packed, plane_here.astype(jnp.int32), field)
    identity = jnp.eye(row_count, dtype=jnp.float32)
    dual_full = identity + dual_part
    calm = jnp.einsum("ay,fyx->fax", dual_full, field[:2, 0], precision=HI)
    calm = lax.all_to_all(calm, "gx", 1, 1, tiled=True)
    fed = jnp.einsum("ay,fyx->fax", dual_full, fed_side, precision=HI)
    fed = lax.all_to_all(fed, "gx", 1, 1, tiled=True)
    tables = dft_tables(gx_count, slab_width)
    position = lax.axis_index("gx")
    eigen_here = lax.dynamic_slice_in_dim(wall_eigen, position * rows_here, rows_here)
    calm = fft_filter(calm, diffusivity[:2], eigen_here, bulk_shift, tables, EXACT)
    calm, fed = lax.optimization_barrier((calm, fed))
    fed = fft_filter(fed, diffusivity[2:], eigen_here, bulk_shift, tables, HI)
    filtered = jnp.concatenate([calm, fed], axis=0)
    filtered = filtered.reshape(field_count, row_count, slab_width)
    gathered = lax.all_to_all(filtered, "gx", 1, 1, tiled=True)
    result = jnp.einsum("fax,ya->fyx", gathered, identity + basis_part, precision=HI)
    return result[:, None]


def solution(mesh):
    in_specs = (
        P(None, "gz", None, "gx"),
        P(("gx", "gz")),
        P(("gx", "gz")),
        P(None, ("gx", "gz")),
        P(),
        P(),
        P(),
        P(),
        P(),
    )
    out_specs = P(None, "gz", None, "gx")
    return jax.shard_map(
        per_device, mesh=mesh, in_specs=in_specs, out_specs=out_specs, check_vma=False
    )
```
